256 devices in a mesh: section: 2 (over core), seq: 16 (over x, y), exp: 8 (over z).
Axes of the slice: x: 4, y: 4, z: 8, core: 2. Of those that a mesh axis runs over, the one named last changes fastest.
Arguments:
- hidden_in: bfloat16 [2048, 2048], P('seq'), may hold values from -6 to 6
- seg_ids: int32 [2048], P('seq'), may hold values from 0 to 7, never falling along the last dimension, each value on 1 to 1024 neighbouring positions
- attn_gain: float32 [2048], replicated, may hold values from 0.25 to 1.75
- w_query: bfloat16 [2048, 2048], P(None, ('section', 'exp'))
- w_key: bfloat16 [2048, 2048], P(None, ('section', 'exp'))
- w_value: bfloat16 [2048, 2048], P(None, ('section', 'exp')), may hold values from -0.125 to 0.125
- w_out: bfloat16 [2048, 2048], P(('section', 'exp')), may hold values from -0.5 to 0.5
- moe_gain: float32 [2048], replicated, may hold values from 0.25 to 1.75
- expert_ids: int32 [2048, 8], P(('seq', 'exp')), may hold values from 0 to 63, all different within a row; in each aligned block of 16 rows (0 to 15, 16 to 31, ...) at most 4 rows name the same one
- route_weights: float32 [2048, 8], P(('seq', 'exp')), may hold values from 0.1 to 0.6
- gate_halves: bfloat16 [128, 2048, 512], P(('seq', 'exp'), None, 'section'), may hold values from -0.125 to 0.125
- up_halves: bfloat16 [128, 2048, 512], P(('seq', 'exp'), None, 'section'), may hold values from -0.125 to 0.125
- down_halves: bfloat16 [128, 512, 2048], P(('seq', 'exp'), 'section'), may hold values from -0.1875 to 0.1875
Outputs:
- layer_out: bfloat16 [2048, 2048], P(('seq', 'exp'))
The draws below stay inside these ranges and needn't reach their ends.
Inputs may be any that keep to these rules, and one draw needn't show every extreme that they name: `seg_ids`: prompt numbers never fall along the batch; each prompt holds 1 to 1024 tokens, and one holds exactly 1024. `expert_ids`: A token's 8 experts are distinct. In each aligned block of 16 tokens (the tokens of one device along seq and exp), no expert is chosen by more than 4 of the block's tokens, a bound that some block reaches.
All inputs are finite; a program needn't handle non-finite values.
Results may differ from the reference program's by a relative error of at most 0.012.
Values may be sent and summed in bfloat16 or wider, within the bound.
No kernel may reach another device: no remote copies, remote signals or barrier semaphores. Data moves between devices by JAX's collectives and lax.ppermute only.
A program may use at most 64 MiB of HBM per device.

```python
import math
import jax
import jax.numpy as jnp
import numpy as np
from jax import lax

D = 2048
FF = 1024
HD = 128
TOPK = 8
TOK_DEV = 16
SEGS = 8
HEADS = 16
EXPERTS = 64
TOKENS = 2048
CAP = 4
PROMPT_MAX = 1024
N_SEQ = 16
N_EXP = 8


def shared_query(key):
    return jax.random.normal(jax.random.fold_in(key, 11), (D, HEADS * HD), jnp.float32)


def draw_w_query(key, part):
    base = shared_query(key)
    return (base * (2.0 / math.sqrt(D))).astype(jnp.bfloat16)


def draw_w_key(key, part):
    fresh = jax.random.normal(jax.random.fold_in(key, 12), (D, HEADS * HD), jnp.float32)
    return (fresh / math.sqrt(D)).astype(jnp.bfloat16)


def block_scale(stream_key, shape, split, smallest, top_value):
    def one(position, shards_of):
        steps = jax.random.uniform(jax.random.fold_in(jax.random.fold_in(stream_key, 6), position), (shards_of,), jnp.float32, smallest / len(split), top_value / len(split))
        return jnp.repeat(jnp.exp(steps), shape[position] // shards_of).reshape((-1,) + (1,) * (len(shape) - position - 1))

    level = one(*split[0])
    for cut in split[1:]:
        level = level * one(*cut)
    return level


def split_up(count, total, most, slope):
    loads = [(1 << 20) // math.isqrt(rank ** slope) + 1 for rank in range(2, count + 1)]
    spare, counts = total - most - (count - 1), [1] * (count - 1)
    while spare > 0:
        movable = [i for i in range(count - 1) if counts[i] < most]
        mass, left = sum([loads[i] for i in movable]), spare
        for i in movable:
            more = min(most - counts[i], max(1, left * loads[i] // mass), spare)
            counts[i] = counts[i] + more
            spare = spare - more
    return np.array([most] + counts)


def uneven(own_key, number_of, total, bound, lean):
    if number_of == 2:
        one = jax.random.randint(own_key, (), max(1, total - bound), min(bound, total - 1) + 1)
        return jnp.stack([one, total - one])
    lengths = jnp.asarray(split_up(number_of, total, bound, lean), jnp.int32)
    twos = (number_of - 1) // 2
    giver, sink = lengths[1:1 + 2 * twos:2], lengths[2:2 + 2 * twos:2]
    slack = jnp.minimum(giver - 1, bound - sink)
    moved = jax.random.randint(jax.random.fold_in(own_key, 1), (twos,), 0, 1 << 20) % (slack + 1)
    lengths = lengths.at[1:1 + 2 * twos:2].set(giver - moved).at[2:2 + 2 * twos:2].set(sink + moved)
    return lengths[jax.random.permutation(jax.random.fold_in(own_key, 2), number_of)]


def deal_out(own_key, own, number, rows, count, top, reach, lean):
    order = jax.random.permutation(own_key, count)
    crowded, common = shares(count, rows * top, reach, lean, True), shares(count, rows * top, reach, lean, False)
    places = jnp.arange(count)

    def named(tallies, turn):
        used = int((tallies > 0).sum())
        fixed = max(1, used // 4)
        passed = fixed + (places - fixed + turn * (used - fixed)) % max(1, count - fixed)
        return jnp.zeros((count,), jnp.int32).at[order[jnp.where(places < fixed, places, passed)]].set(jnp.asarray(tallies, jnp.int32))

    tallies = jnp.where(number % 4 == 0, named(crowded, number // 4), named(common, number - number // 4 - 1))
    mixed = jax.random.permutation(jax.random.fold_in(own, 3), count)
    giver, receiver = mixed[0:count // 2 * 2:2], mixed[1:count // 2 * 2:2]
    slack = jnp.minimum(tallies[giver] - 1, reach - tallies[receiver]) // 2
    slack = jnp.where((giver == order[0]) | (receiver == order[0]) | (tallies[receiver] == 0), 0, jnp.maximum(slack, 0))
    passed = jax.random.randint(jax.random.fold_in(own, 4), (count // 2,), 0, 1 << 20) % (slack + 1)
    tallies = tallies.at[giver].add(-passed).at[receiver].add(passed)
    members = jnp.searchsorted(jnp.cumsum(tallies), jnp.arange(rows * top), side="right").astype(jnp.int32)
    listing = members.reshape(top, rows).T
    listing = listing[jax.random.permutation(jax.random.fold_in(own, 1), rows)]
    turn = jax.random.randint(jax.random.fold_in(own, 2), (rows, 1), 0, top)
    return jnp.take_along_axis(listing, (jnp.arange(top)[None, :] + turn) % top, axis=1)


def shares(amount, total, limit, lean, full):
    portions = [(1 << 20) // math.isqrt(grade ** lean) + 1 for grade in range(1, amount + 1)]
    largest = limit if full else min(limit, max(-(-total // amount), total * portions[0] // sum(portions)))
    least = 1 if total - largest >= amount - 1 else 0
    holding, rest = [largest] + [least] * (amount - 1), total - largest - least * (amount - 1)
    while rest > 0:
        movable = [i for i in range(1, amount) if holding[i] < largest] or [i for i in range(1, amount) if holding[i] < limit]
        mass, remaining = sum([portions[i] for i in movable]), rest
        for i in movable:
            more = min(limit - holding[i], max(1, remaining * portions[i] // mass), rest)
            holding[i] = holding[i] + more
            rest = rest - more
    return np.array(holding)


def scatter_about(own_key, extent, scale, most, split=(), kind=jnp.bfloat16):
    drawn = jax.random.normal(own_key, extent, jnp.float32) * scale
    if len(split) > 0:
        drawn = block_scale(own_key, extent, split, -0.22, 0.18) * drawn
    return jnp.clip(drawn, min=-most, max=most).astype(kind)


def setup_inputs(seed: int = 0) -> dict:
    splits = jax.random.split(jax.random.key(seed), 14)
    hidden_in = scatter_about(splits[0], (TOKENS, D), 1.0, 6.0, ((0, 16),))
    seg_ids = jnp.searchsorted(jnp.cumsum(uneven(splits[1], SEGS, TOKENS, PROMPT_MAX, 2)), jnp.arange(TOKENS), side="right").astype(jnp.int32)
    attn_gain = jnp.clip(1.0 + 0.15 * jax.random.normal(splits[2], (D,), jnp.float32), 0.25, 1.75)
    w_query = draw_w_query(jax.random.fold_in(splits[13], 71), 0)
    w_key = draw_w_key(jax.random.fold_in(splits[13], 71), 0)
    w_value = scatter_about(splits[5], (D, HEADS * HD), D ** -0.5, 0.125, ((1, 16),))
    w_out = scatter_about(splits[6], (HEADS * HD, D), HD ** -0.5, 0.5, ((0, 16),))
    moe_gain = jnp.clip(1.0 + 0.15 * jax.random.normal(splits[7], (D,), jnp.float32), 0.25, 1.75)
    expert_ids_keys = jax.random.split(jax.random.fold_in(splits[8], 1), TOKENS // TOK_DEV)
    expert_ids_turns = jax.random.permutation(jax.random.fold_in(splits[8], 3), TOKENS // TOK_DEV)
    expert_ids = jax.vmap(lambda own, number: deal_out(jax.random.fold_in(splits[8], 2), own, number, TOK_DEV, EXPERTS, TOPK, CAP, 2))(expert_ids_keys, expert_ids_turns).reshape((TOKENS, TOPK))
    route_weights = jnp.clip(jnp.exp(math.log(0.6) - 1.7917595 * jax.random.uniform(splits[9], (TOKENS, TOPK), jnp.float32) ** block_scale(splits[9], (TOKENS, TOPK), ((0, 128),), -0.2, 0.2)), 0.1, 0.6)
    gate_halves = scatter_about(splits[10], (2 * EXPERTS, D, FF // 2), D ** -0.5, 0.125, ((0, 128), (2, 2)))
    up_halves = scatter_about(splits[11], (2 * EXPERTS, D, FF // 2), D ** -0.5, 0.125, ((0, 128), (2, 2)))
    down_halves = scatter_about(splits[12], (2 * EXPERTS, FF // 2, D), FF ** -0.5, 0.1875, ((0, 128), (1, 2)))
    return dict(hidden_in=hidden_in, seg_ids=seg_ids, attn_gain=attn_gain, w_query=w_query, w_key=w_key, w_value=w_value, w_out=w_out, moe_gain=moe_gain, expert_ids=expert_ids, route_weights=route_weights, gate_halves=gate_halves, up_halves=up_halves, down_halves=down_halves)


epsilon = 1e-05
rope_base = 10000.0

def rms_scale(rows, gain):
    wide = rows.astype(jnp.float32)
    inverse = lax.rsqrt(lax.optimization_barrier(jnp.mean(wide * wide, axis=-1, keepdims=True)) + epsilon)
    return (wide * inverse * gain).astype(jnp.bfloat16)

def rotate(values, positions):
    half_dim = values.shape[-1] // 2
    frequency = rope_base ** (-2.0 * jnp.arange(half_dim, dtype=jnp.float32) / values.shape[-1])
    angles = positions.astype(jnp.float32)[:, None] * frequency[None, :]
    cosine = jnp.cos(angles)
    sine_part = jnp.sin(angles)
    first_half = values[:, :half_dim]
    second_half = values[:, half_dim:]
    return jnp.concatenate([first_half * cosine - second_half * sine_part, second_half * cosine + first_half * sine_part], axis=-1)

def reference(hidden_in, seg_ids, attn_gain, w_query, w_key, w_value, w_out, moe_gain, expert_ids, route_weights, gate_halves, up_halves, down_halves):
    positions = jnp.arange(TOKENS, dtype=jnp.int32)
    normed = rms_scale(hidden_in, attn_gain)
    allowed = (seg_ids[:, None] == seg_ids[None, :]) & (positions[None, :] <= positions[:, None])
    score_scale = 1.0 / math.sqrt(HD)

    def one_head(carry, head_index):
        columns = head_index * HD
        query_rows = rotate(jnp.dot(normed, lax.dynamic_slice_in_dim(w_query, columns, HD, 1), preferred_element_type=jnp.float32), positions).astype(jnp.bfloat16)
        key_rows = rotate(jnp.dot(normed, lax.dynamic_slice_in_dim(w_key, columns, HD, 1), preferred_element_type=jnp.float32), positions).astype(jnp.bfloat16)
        value_rows = jnp.dot(normed, lax.dynamic_slice_in_dim(w_value, columns, HD, 1), preferred_element_type=jnp.float32).astype(jnp.bfloat16)
        scores = jnp.dot(query_rows, key_rows.T, preferred_element_type=jnp.float32) * score_scale
        masked = jnp.where(allowed, scores, -1e+30)
        row_max = lax.optimization_barrier(jnp.max(masked, axis=1, keepdims=True))
        weights = jnp.where(allowed, jnp.exp(masked - row_max), 0.0)
        row_total = lax.optimization_barrier(jnp.sum(weights, axis=1, keepdims=True))
        head_out = (jnp.dot(weights.astype(jnp.bfloat16), value_rows, preferred_element_type=jnp.float32) / row_total).astype(jnp.bfloat16)
        out_rows = lax.dynamic_slice_in_dim(w_out, columns, HD, 0)
        return (carry + jnp.dot(head_out, out_rows, preferred_element_type=jnp.float32), None)
    attn_sum, unused = lax.scan(one_head, jnp.zeros((TOKENS, D), jnp.float32), jnp.arange(HEADS, dtype=jnp.int32))
    residual = (hidden_in.astype(jnp.float32) + attn_sum).astype(jnp.bfloat16)
    moe_in = rms_scale(residual, moe_gain)
    quarter = FF // 4
    rows_cap = min(TOKENS, N_SEQ * N_EXP * CAP)
    token_index = jnp.arange(TOKENS, dtype=jnp.int32)

    def one_expert(carry, expert):
        chosen = expert_ids == expert
        weight_rows = lax.optimization_barrier(jnp.sum(jnp.where(chosen, route_weights, 0.0), axis=1))
        order_key = jnp.where(jnp.any(chosen, axis=1), token_index, TOKENS + token_index)
        picked = jnp.argsort(order_key)[:rows_cap].astype(jnp.int32)
        rows = moe_in[picked]
        expert_out = jnp.zeros((rows_cap, D), jnp.float32)
        for half_index in range(2):
            gate_full = lax.dynamic_index_in_dim(gate_halves, 2 * expert + half_index, 0, keepdims=False)
            up_full = lax.dynamic_index_in_dim(up_halves, 2 * expert + half_index, 0, keepdims=False)
            down_full = lax.dynamic_index_in_dim(down_halves, 2 * expert + half_index, 0, keepdims=False)
            for part_index in range(2):
                lower = part_index * quarter
                gate_proj = jnp.dot(rows, gate_full[:, lower:lower + quarter], preferred_element_type=jnp.float32)
                up_proj = jnp.dot(rows, up_full[:, lower:lower + quarter], preferred_element_type=jnp.float32)
                activated = (jax.nn.silu(gate_proj) * up_proj).astype(jnp.bfloat16)
                quarter_out = jnp.dot(activated, down_full[lower:lower + quarter, :], preferred_element_type=jnp.float32)
                expert_out = expert_out + lax.optimization_barrier(quarter_out.astype(jnp.bfloat16)).astype(jnp.float32)
        return (carry.at[picked].add(expert_out * weight_rows[picked][:, None]), None)
    moe_total, unused = lax.scan(one_expert, jnp.zeros((TOKENS, D), jnp.float32), jnp.arange(EXPERTS, dtype=jnp.int32))
    return (residual.astype(jnp.float32) + moe_total).astype(jnp.bfloat16)
```

```python
import math

import jax
import jax.numpy as jnp
from jax import lax
from jax.sharding import PartitionSpec as P

epsilon = 1e-05
rope_base = 10000.0


def rms_scale(rows, gain):
    wide = rows.astype(jnp.float32)
    inverse = lax.rsqrt(jnp.mean(wide * wide, axis=-1, keepdims=True) + epsilon)
    return (wide * inverse * gain).astype(jnp.bfloat16)


def rotate(values, positions):
    half_dim = values.shape[-1] // 2
    frequency = rope_base ** (-2.0 * jnp.arange(half_dim, dtype=jnp.float32) / values.shape[-1])
    angles = positions.astype(jnp.float32)[:, None] * frequency[None, :]
    cosine = jnp.cos(angles)
    sine_part = jnp.sin(angles)
    first_half = values[:, :half_dim]
    second_half = values[:, half_dim:]
    return jnp.concatenate(
        [
            first_half * cosine - second_half * sine_part,
            second_half * cosine + first_half * sine_part,
        ],
        axis=-1,
    )


def per_device(
    hidden_in,
    seg_ids,
    attn_gain,
    w_query,
    w_key,
    w_value,
    w_out,
    moe_gain,
    expert_ids,
    route_weights,
    gate_halves,
    up_halves,
    down_halves,
):
    tok_seq = hidden_in.shape[0]
    width = hidden_in.shape[1]
    head_dim = w_query.shape[1]
    positions = lax.axis_index("seq") * tok_seq + jnp.arange(tok_seq, dtype=jnp.int32)
    normed = rms_scale(hidden_in, attn_gain)
    query_rows = rotate(
        jnp.dot(normed, w_query, preferred_element_type=jnp.float32), positions
    ).astype(jnp.bfloat16)
    key_rows = rotate(jnp.dot(normed, w_key, preferred_element_type=jnp.float32), positions).astype(
        jnp.bfloat16
    )
    value_rows = jnp.dot(normed, w_value, preferred_element_type=jnp.float32).astype(jnp.bfloat16)
    score_scale = 1.0 / math.sqrt(head_dim)
    run_max = jnp.full((tok_seq,), -1e30, jnp.float32)
    seg_block = jnp.broadcast_to(seg_ids.astype(jnp.bfloat16)[:, None], (tok_seq, head_dim))
    packed = jnp.concatenate([key_rows, value_rows, seg_block], axis=1)
    gathered = lax.all_gather(packed, "seq", axis=0, tiled=True)
    piece_keys = gathered[:, :head_dim]
    piece_values = gathered[:, head_dim : 2 * head_dim]
    key_segs = gathered[:, 2 * head_dim].astype(jnp.int32)
    piece_rows = piece_keys.shape[0]
    scores = (
        lax.dot_general(
            query_rows, piece_keys, (((1,), (1,)), ((), ())), preferred_element_type=jnp.float32
        )
        * score_scale
    )
    key_pos = jnp.arange(piece_rows, dtype=jnp.int32)
    allowed = (seg_ids[:, None] == key_segs[None, :]) & (key_pos[None, :] <= positions[:, None])
    masked = jnp.where(allowed, scores, -1e30)
    new_max = jnp.maximum(run_max, jnp.max(masked, axis=1))
    weights = jnp.where(allowed, jnp.exp(masked - new_max[:, None]), 0.0)
    run_total = jnp.sum(weights, axis=1)
    weighted_sum = jnp.dot(
        weights.astype(jnp.bfloat16), piece_values, preferred_element_type=jnp.float32
    )
    run_max, run_total, weighted_sum = (new_max, run_total, weighted_sum)
    head_out = (weighted_sum / run_total[:, None]).astype(jnp.bfloat16)
    partial_value = jnp.dot(head_out, w_out, preferred_element_type=jnp.float32)
    tok_dev = tok_seq // lax.axis_size("exp")
    own_start = lax.axis_index("exp") * tok_dev
    summed = lax.psum_scatter(partial_value, "exp", scatter_dimension=0, tiled=True)
    summed = summed + lax.ppermute(summed, "section", [(0, 1), (1, 0)])
    own_rows = lax.dynamic_slice_in_dim(hidden_in, own_start, tok_dev, 0)
    residual = (own_rows.astype(jnp.float32) + summed).astype(jnp.bfloat16)
    moe_in = rms_scale(residual, moe_gain)
    experts = lax.axis_size("seq") * lax.axis_size("exp") // 2
    top_count = expert_ids.shape[1]
    capacity = min(tok_dev, max(2, 2 * tok_dev * top_count // experts))
    row_count = tok_dev * top_count
    flat_ids = expert_ids.reshape(row_count)
    one_hot = (flat_ids[:, None] == jnp.arange(experts, dtype=jnp.int32)[None, :]).astype(jnp.int32)
    slot_rank = jnp.sum((jnp.cumsum(one_hot, axis=0) - one_hot) * one_hot, axis=1)
    slot_index = flat_ids * capacity + slot_rank
    placed = slot_index[:, None] == jnp.arange(experts * capacity, dtype=jnp.int32)[None, :]
    repeated = jnp.repeat(moe_in, top_count, axis=0)
    outgoing = lax.dot_general(
        placed.astype(jnp.bfloat16),
        repeated,
        (((0,), (0,)), ((), ())),
        preferred_element_type=jnp.float32,
    ).astype(jnp.bfloat16)
    row_token = jnp.arange(row_count, dtype=jnp.int32) // top_count
    token_hot = (row_token[None, :] == jnp.arange(tok_dev, dtype=jnp.int32)[:, None]).astype(
        jnp.float32
    )
    weighted = token_hot * route_weights.reshape(row_count)[None, :]
    combine = jnp.dot(weighted, placed.astype(jnp.float32), precision=lax.Precision.HIGHEST)
    doubled = jnp.broadcast_to(
        outgoing.reshape(experts, 1, capacity, width), (experts, 2, capacity, width)
    ).reshape(2 * experts, capacity, width)
    arrived = lax.all_to_all(doubled, ("seq", "exp"), split_axis=0, concat_axis=0, tiled=True)
    flat_rows = arrived.reshape(-1, width)
    gate_proj = jnp.dot(flat_rows, gate_halves[0], preferred_element_type=jnp.float32)
    up_proj = jnp.dot(flat_rows, up_halves[0], preferred_element_type=jnp.float32)
    activated = (jax.nn.silu(gate_proj) * up_proj).astype(jnp.bfloat16)
    returned = lax.all_to_all(
        jnp.dot(activated, down_halves[0], preferred_element_type=jnp.float32)
        .astype(jnp.bfloat16)
        .reshape(arrived.shape),
        ("seq", "exp"),
        split_axis=0,
        concat_axis=0,
        tiled=True,
    )
    halves_sum = jnp.sum(
        returned.reshape(experts, 2, capacity, width).astype(jnp.float32), axis=1
    ).reshape(experts * capacity, width)
    moe_part = jnp.dot(combine, halves_sum, precision=lax.Precision.HIGHEST)
    moe_total = moe_part + lax.ppermute(moe_part, "section", [(0, 1), (1, 0)])
    return (residual.astype(jnp.float32) + moe_total).astype(jnp.bfloat16)


def solution(mesh):
    in_specs = (
        P("seq", None),
        P("seq"),
        P(),
        P(None, ("section", "exp")),
        P(None, ("section", "exp")),
        P(None, ("section", "exp")),
        P(("section", "exp"), None),
        P(),
        P(("seq", "exp"), None),
        P(("seq", "exp"), None),
        P(("seq", "exp"), None, "section"),
        P(("seq", "exp"), None, "section"),
        P(("seq", "exp"), "section", None),
    )
    out_specs = P(("seq", "exp"), None)
    return jax.shard_map(
        per_device, mesh=mesh, in_specs=in_specs, out_specs=out_specs, check_vma=False
    )
```

```python
import math

import jax
import jax.numpy as jnp
from jax import lax
from jax.sharding import PartitionSpec as P

epsilon = 1e-05
rope_base = 10000.0
prompt_max = 1024


def rms_scale(rows, gain):
    wide = rows.astype(jnp.float32)
    inverse = lax.rsqrt(jnp.mean(wide * wide, axis=-1, keepdims=True) + epsilon)
    return (wide * inverse * gain).astype(jnp.bfloat16)


def rotate(values, positions):
    half_dim = values.shape[-1] // 2
    frequency = rope_base ** (-2.0 * jnp.arange(half_dim, dtype=jnp.float32) / values.shape[-1])
    angles = positions.astype(jnp.float32)[:, None] * frequency[None, :]
    cosine = jnp.cos(angles)
    sine_part = jnp.sin(angles)
    first_half = values[:, :half_dim]
    second_half = values[:, half_dim:]
    return jnp.concatenate(
        [
            first_half * cosine - second_half * sine_part,
            second_half * cosine + first_half * sine_part,
        ],
        axis=-1,
    )


def per_device(
    hidden_in,
    seg_ids,
    attn_gain,
    w_query,
    w_key,
    w_value,
    w_out,
    moe_gain,
    expert_ids,
    route_weights,
    gate_halves,
    up_halves,
    down_halves,
):
    tok_seq = hidden_in.shape[0]
    width = hidden_in.shape[1]
    head_dim = w_query.shape[1]
    positions = lax.axis_index("seq") * tok_seq + jnp.arange(tok_seq, dtype=jnp.int32)
    normed = rms_scale(hidden_in, attn_gain)
    query_rows = rotate(
        jnp.dot(normed, w_query, preferred_element_type=jnp.float32), positions
    ).astype(jnp.bfloat16)
    key_rows = rotate(jnp.dot(normed, w_key, preferred_element_type=jnp.float32), positions).astype(
        jnp.bfloat16
    )
    value_rows = jnp.dot(normed, w_value, preferred_element_type=jnp.float32).astype(jnp.bfloat16)
    score_scale = 1.0 / math.sqrt(head_dim)
    run_max = jnp.full((tok_seq,), -1e30, jnp.float32)
    n_seq = lax.axis_size("seq")
    seq_index = lax.axis_index("seq")
    window = min(n_seq - 1, -(-(prompt_max - 1) // tok_seq))
    packed = jnp.concatenate([key_rows, value_rows], axis=1)
    got_rows = [packed]
    got_segs = [seg_ids]
    for shift in range(1, window + 1):
        pairs = [(j, j + shift) for j in range(n_seq - shift)]
        rows, segs = lax.ppermute((packed, seg_ids), "seq", pairs)
        got_rows.append(rows)
        got_segs.append(segs)
    gathered = jnp.concatenate(got_rows, axis=0)
    piece_keys = gathered[:, :head_dim]
    piece_values = gathered[:, head_dim:]
    key_segs = jnp.concatenate(got_segs, axis=0)
    piece_rows = piece_keys.shape[0]
    scores = (
        lax.dot_general(
            query_rows, piece_keys, (((1,), (1,)), ((), ())), preferred_element_type=jnp.float32
        )
        * score_scale
    )
    key_piece = seq_index - jnp.arange(piece_rows, dtype=jnp.int32) // tok_seq
    key_pos = key_piece * tok_seq + jnp.arange(piece_rows, dtype=jnp.int32) % tok_seq
    allowed = (
        (seg_ids[:, None] == key_segs[None, :])
        & (key_pos[None, :] <= positions[:, None])
        & (key_piece[None, :] >= 0)
    )
    masked = jnp.where(allowed, scores, -1e30)
    new_max = jnp.maximum(run_max, jnp.max(masked, axis=1))
    weights = jnp.where(allowed, jnp.exp(masked - new_max[:, None]), 0.0)
    run_total = jnp.sum(weights, axis=1)
    weighted_sum = jnp.dot(
        weights.astype(jnp.bfloat16), piece_values, preferred_element_type=jnp.float32
    )
    run_max, run_total, weighted_sum = (new_max, run_total, weighted_sum)
    head_out = (weighted_sum / run_total[:, None]).astype(jnp.bfloat16)
    partial_value = jnp.dot(head_out, w_out, preferred_element_type=jnp.float32)
    tok_dev = tok_seq // lax.axis_size("exp")
    own_start = lax.axis_index("exp") * tok_dev
    n_exp = lax.axis_size("exp")
    exp_index = lax.axis_index("exp")
    summed = lax.dynamic_slice_in_dim(partial_value, own_start, tok_dev, 0)
    for shift in range(1, n_exp):
        target = (exp_index + shift) % n_exp
        chunk = lax.dynamic_slice_in_dim(partial_value, target * tok_dev, tok_dev, 0)
        pairs = [(j, (j + shift) % n_exp) for j in range(n_exp)]
        summed = summed + lax.ppermute(chunk, "exp", pairs)
    summed = summed + lax.ppermute(summed, "section", [(0, 1), (1, 0)])
    own_rows = lax.dynamic_slice_in_dim(hidden_in, own_start, tok_dev, 0)
    residual = (own_rows.astype(jnp.float32) + summed).astype(jnp.bfloat16)
    moe_in = rms_scale(residual, moe_gain)
    experts = lax.axis_size("seq") * lax.axis_size("exp") // 2
    top_count = expert_ids.shape[1]
    capacity = min(tok_dev, max(2, 2 * tok_dev * top_count // experts))
    row_count = tok_dev * top_count
    flat_ids = expert_ids.reshape(row_count)
    one_hot = (flat_ids[:, None] == jnp.arange(experts, dtype=jnp.int32)[None, :]).astype(jnp.int32)
    slot_rank = jnp.sum((jnp.cumsum(one_hot, axis=0) - one_hot) * one_hot, axis=1)
    slot_index = flat_ids * capacity + slot_rank
    placed = slot_index[:, None] == jnp.arange(experts * capacity, dtype=jnp.int32)[None, :]
    repeated = jnp.repeat(moe_in, top_count, axis=0)
    outgoing = lax.dot_general(
        placed.astype(jnp.bfloat16),
        repeated,
        (((0,), (0,)), ((), ())),
        preferred_element_type=jnp.float32,
    ).astype(jnp.bfloat16)
    row_token = jnp.arange(row_count, dtype=jnp.int32) // top_count
    token_hot = (row_token[None, :] == jnp.arange(tok_dev, dtype=jnp.int32)[:, None]).astype(
        jnp.float32
    )
    weighted = token_hot * route_weights.reshape(row_count)[None, :]
    combine = jnp.dot(weighted, placed.astype(jnp.float32), precision=lax.Precision.HIGHEST)
    doubled = jnp.broadcast_to(
        outgoing.reshape(experts, 1, capacity, width), (experts, 2, capacity, width)
    ).reshape(2 * experts, capacity, width)
    arrived = lax.all_to_all(doubled, ("seq", "exp"), split_axis=0, concat_axis=0, tiled=True)
    flat_rows = arrived.reshape(-1, width)
    gate_proj = jnp.dot(flat_rows, gate_halves[0], preferred_element_type=jnp.float32)
    up_proj = jnp.dot(flat_rows, up_halves[0], preferred_element_type=jnp.float32)
    activated = (jax.nn.silu(gate_proj) * up_proj).astype(jnp.bfloat16)
    returned = lax.all_to_all(
        jnp.dot(activated, down_halves[0], preferred_element_type=jnp.float32)
        .astype(jnp.bfloat16)
        .reshape(arrived.shape),
        ("seq", "exp"),
        split_axis=0,
        concat_axis=0,
        tiled=True,
    )
    halves_sum = jnp.sum(
        returned.reshape(experts, 2, capacity, width).astype(jnp.float32), axis=1
    ).reshape(experts * capacity, width)
    moe_part = jnp.dot(combine, halves_sum, precision=lax.Precision.HIGHEST)
    moe_total = moe_part + lax.ppermute(moe_part, "section", [(0, 1), (1, 0)])
    return (residual.astype(jnp.float32) + moe_total).astype(jnp.bfloat16)


def solution(mesh):
    in_specs = (
        P("seq", None),
        P("seq"),
        P(),
        P(None, ("section", "exp")),
        P(None, ("section", "exp")),
        P(None, ("section", "exp")),
        P(("section", "exp"), None),
        P(),
        P(("seq", "exp"), None),
        P(("seq", "exp"), None),
        P(("seq", "exp"), None, "section"),
        P(("seq", "exp"), None, "section"),
        P(("seq", "exp"), "section", None),
    )
    out_specs = P(("seq", "exp"), None)
    return jax.shard_map(
        per_device, mesh=mesh, in_specs=in_specs, out_specs=out_specs, check_vma=False
    )
```

```python
import math

import jax
import jax.numpy as jnp
from jax import lax
from jax.sharding import PartitionSpec as P

epsilon = 1e-05
rope_base = 10000.0
prompt_max = 1024


def rms_scale(rows, gain):
    wide = rows.astype(jnp.float32)
    inverse = lax.rsqrt(jnp.mean(wide * wide, axis=-1, keepdims=True) + epsilon)
    return (wide * inverse * gain).astype(jnp.bfloat16)


def rotate(values, positions):
    half_dim = values.shape[-1] // 2
    frequency = rope_base ** (-2.0 * jnp.arange(half_dim, dtype=jnp.float32) / values.shape[-1])
    angles = positions.astype(jnp.float32)[:, None] * frequency[None, :]
    cosine = jnp.cos(angles)
    sine_part = jnp.sin(angles)
    first_half = values[:, :half_dim]
    second_half = values[:, half_dim:]
    return jnp.concatenate(
        [
            first_half * cosine - second_half * sine_part,
            second_half * cosine + first_half * sine_part,
        ],
        axis=-1,
    )


def per_device(
    hidden_in,
    seg_ids,
    attn_gain,
    w_query,
    w_key,
    w_value,
    w_out,
    moe_gain,
    expert_ids,
    route_weights,
    gate_halves,
    up_halves,
    down_halves,
):
    tok_seq = hidden_in.shape[0]
    width = hidden_in.shape[1]
    head_dim = w_query.shape[1]
    positions = lax.axis_index("seq") * tok_seq + jnp.arange(tok_seq, dtype=jnp.int32)
    normed = rms_scale(hidden_in, attn_gain)
    query_rows = rotate(
        jnp.dot(normed, w_query, preferred_element_type=jnp.float32), positions
    ).astype(jnp.bfloat16)
    key_rows = rotate(jnp.dot(normed, w_key, preferred_element_type=jnp.float32), positions).astype(
        jnp.bfloat16
    )
    value_rows = jnp.dot(normed, w_value, preferred_element_type=jnp.float32).astype(jnp.bfloat16)
    score_scale = 1.0 / math.sqrt(head_dim)
    run_max = jnp.full((tok_seq,), -1e30, jnp.float32)
    n_seq = lax.axis_size("seq")
    seq_index = lax.axis_index("seq")
    window = min(n_seq - 1, -(-(prompt_max - 1) // tok_seq))
    seg_rows = jnp.zeros((16, 2 * head_dim), jnp.bfloat16)
    seg_rows = seg_rows.at[0, :tok_seq].set(seg_ids.astype(jnp.bfloat16))
    packed = jnp.concatenate([jnp.concatenate([key_rows, value_rows], axis=1), seg_rows], axis=0)
    got = [packed]
    for shift in range(1, window + 1):
        pairs = [(j, j + shift) for j in range(n_seq - shift)]
        got.append(lax.ppermute(packed, "seq", pairs))
    gathered = jnp.stack(got, axis=0)
    piece_keys = gathered[:, :tok_seq, :head_dim].reshape(-1, head_dim)
    piece_values = gathered[:, :tok_seq, head_dim:].reshape(-1, head_dim)
    key_segs = gathered[:, tok_seq, :tok_seq].reshape(-1).astype(jnp.int32)
    piece_rows = piece_keys.shape[0]
    scores = (
        lax.dot_general(
            query_rows, piece_keys, (((1,), (1,)), ((), ())), preferred_element_type=jnp.float32
        )
        * score_scale
    )
    key_piece = seq_index - jnp.arange(piece_rows, dtype=jnp.int32) // tok_seq
    key_pos = key_piece * tok_seq + jnp.arange(piece_rows, dtype=jnp.int32) % tok_seq
    allowed = (
        (seg_ids[:, None] == key_segs[None, :])
        & (key_pos[None, :] <= positions[:, None])
        & (key_piece[None, :] >= 0)
    )
    masked = jnp.where(allowed, scores, -1e30)
    new_max = jnp.maximum(run_max, jnp.max(masked, axis=1))
    weights = jnp.where(allowed, jnp.exp(masked - new_max[:, None]), 0.0)
    run_total = jnp.sum(weights, axis=1)
    weighted_sum = jnp.dot(
        weights.astype(jnp.bfloat16), piece_values, preferred_element_type=jnp.float32
    )
    run_max, run_total, weighted_sum = (new_max, run_total, weighted_sum)
    head_out = (weighted_sum / run_total[:, None]).astype(jnp.bfloat16)
    partial_value = jnp.dot(head_out, w_out, preferred_element_type=jnp.float32)
    tok_dev = tok_seq // lax.axis_size("exp")
    own_start = lax.axis_index("exp") * tok_dev
    n_exp = lax.axis_size("exp")
    exp_index = lax.axis_index("exp")
    summed = lax.dynamic_slice_in_dim(partial_value, own_start, tok_dev, 0)
    for shift in range(1, n_exp):
        target = (exp_index + shift) % n_exp
        chunk = lax.dynamic_slice_in_dim(partial_value, target * tok_dev, tok_dev, 0)
        pairs = [(j, (j + shift) % n_exp) for j in range(n_exp)]
        summed = summed + lax.ppermute(chunk, "exp", pairs)
    summed = summed + lax.ppermute(summed, "section", [(0, 1), (1, 0)])
    own_rows = lax.dynamic_slice_in_dim(hidden_in, own_start, tok_dev, 0)
    residual = (own_rows.astype(jnp.float32) + summed).astype(jnp.bfloat16)
    moe_in = rms_scale(residual, moe_gain)
    experts = lax.axis_size("seq") * lax.axis_size("exp") // 2
    top_count = expert_ids.shape[1]
    capacity = min(tok_dev, max(2, 2 * tok_dev * top_count // experts))
    row_count = tok_dev * top_count
    flat_ids = expert_ids.reshape(row_count)
    one_hot = (flat_ids[:, None] == jnp.arange(experts, dtype=jnp.int32)[None, :]).astype(jnp.int32)
    slot_rank = jnp.sum((jnp.cumsum(one_hot, axis=0) - one_hot) * one_hot, axis=1)
    slot_index = flat_ids * capacity + slot_rank
    placed = slot_index[:, None] == jnp.arange(experts * capacity, dtype=jnp.int32)[None, :]
    repeated = jnp.repeat(moe_in, top_count, axis=0)
    outgoing = lax.dot_general(
        placed.astype(jnp.bfloat16),
        repeated,
        (((0,), (0,)), ((), ())),
        preferred_element_type=jnp.float32,
    ).astype(jnp.bfloat16)
    row_token = jnp.arange(row_count, dtype=jnp.int32) // top_count
    token_hot = (row_token[None, :] == jnp.arange(tok_dev, dtype=jnp.int32)[:, None]).astype(
        jnp.float32
    )
    weighted = token_hot * route_weights.reshape(row_count)[None, :]
    combine = jnp.dot(weighted, placed.astype(jnp.float32), precision=lax.Precision.HIGHEST)
    section_index = lax.axis_index("section")
    half_cap = capacity // 2
    own_half = lax.dynamic_slice_in_dim(
        outgoing.reshape(experts, capacity, width), section_index * half_cap, half_cap, 1
    )
    doubled = jnp.broadcast_to(
        own_half.reshape(experts, 1, half_cap, width), (experts, 2, half_cap, width)
    ).reshape(2 * experts, half_cap, width)
    arrived = lax.all_to_all(doubled, ("seq", "exp"), split_axis=0, concat_axis=0, tiled=True)
    partner = lax.ppermute(arrived, "section", [(0, 1), (1, 0)])
    flat_rows = jnp.concatenate([arrived, partner], axis=0).reshape(-1, width)
    gate_proj = jnp.dot(flat_rows, gate_halves[0], preferred_element_type=jnp.float32)
    up_proj = jnp.dot(flat_rows, up_halves[0], preferred_element_type=jnp.float32)
    activated = (jax.nn.silu(gate_proj) * up_proj).astype(jnp.bfloat16)
    quarter_out = jnp.dot(activated, down_halves[0], preferred_element_type=jnp.float32).astype(
        jnp.bfloat16
    )
    own_rows_out = quarter_out[: arrived.shape[0] * half_cap]
    partner_rows_out = quarter_out[arrived.shape[0] * half_cap :]
    pair_sum = own_rows_out.astype(jnp.float32) + lax.ppermute(
        partner_rows_out, "section", [(0, 1), (1, 0)]
    ).astype(jnp.float32)
    returned = lax.all_to_all(
        pair_sum.astype(jnp.bfloat16).reshape(arrived.shape),
        ("seq", "exp"),
        split_axis=0,
        concat_axis=0,
        tiled=True,
    )
    halves_sum = jnp.sum(
        returned.reshape(experts, 2, half_cap, width).astype(jnp.float32), axis=1
    ).reshape(experts * half_cap, width)
    own_combine = lax.dynamic_slice_in_dim(
        combine.reshape(tok_dev, experts, capacity), section_index * half_cap, half_cap, 2
    ).reshape(tok_dev, experts * half_cap)
    moe_part = jnp.dot(own_combine, halves_sum, precision=lax.Precision.HIGHEST)
    moe_total = moe_part + lax.ppermute(moe_part, "section", [(0, 1), (1, 0)])
    return (residual.astype(jnp.float32) + moe_total).astype(jnp.bfloat16)


def solution(mesh):
    in_specs = (
        P("seq", None),
        P("seq"),
        P(),
        P(None, ("section", "exp")),
        P(None, ("section", "exp")),
        P(None, ("section", "exp")),
        P(("section", "exp"), None),
        P(),
        P(("seq", "exp"), None),
        P(("seq", "exp"), None),
        P(("seq", "exp"), None, "section"),
        P(("seq", "exp"), None, "section"),
        P(("seq", "exp"), "section", None),
    )
    out_specs = P(("seq", "exp"), None)
    return jax.shard_map(
        per_device, mesh=mesh, in_specs=in_specs, out_specs=out_specs, check_vma=False
    )
```

```python
import math

import jax
import jax.numpy as jnp
from jax import lax
from jax.sharding import PartitionSpec as P

epsilon = 1e-05
rope_base = 10000.0
prompt_max = 1024


def rms_scale(rows, gain):
    wide = rows.astype(jnp.float32)
    inverse = lax.rsqrt(jnp.mean(wide * wide, axis=-1, keepdims=True) + epsilon)
    return (wide * inverse * gain).astype(jnp.bfloat16)


def rotate(values, positions):
    half_dim = values.shape[-1] // 2
    frequency = rope_base ** (-2.0 * jnp.arange(half_dim, dtype=jnp.float32) / values.shape[-1])
    angles = positions.astype(jnp.float32)[:, None] * frequency[None, :]
    cosine = jnp.cos(angles)
    sine_part = jnp.sin(angles)
    first_half = values[:, :half_dim]
    second_half = values[:, half_dim:]
    return jnp.concatenate(
        [
            first_half * cosine - second_half * sine_part,
            second_half * cosine + first_half * sine_part,
        ],
        axis=-1,
    )


def two_stage_all_to_all(blocks):
    n_seq = lax.axis_size("seq")
    n_exp = lax.axis_size("exp")
    rest = blocks.shape[1:]
    grid = blocks.reshape((n_seq, n_exp) + rest)
    grid = lax.all_to_all(grid, "exp", split_axis=1, concat_axis=1, tiled=True)
    grid = lax.all_to_all(grid, "seq", split_axis=0, concat_axis=0, tiled=True)
    return grid.reshape(blocks.shape)


def per_device(
    hidden_in,
    seg_ids,
    attn_gain,
    w_query,
    w_key,
    w_value,
    w_out,
    moe_gain,
    expert_ids,
    route_weights,
    gate_halves,
    up_halves,
    down_halves,
):
    tok_seq = hidden_in.shape[0]
    width = hidden_in.shape[1]
    head_dim = w_query.shape[1]
    positions = lax.axis_index("seq") * tok_seq + jnp.arange(tok_seq, dtype=jnp.int32)
    normed = rms_scale(hidden_in, attn_gain)
    query_rows = rotate(
        jnp.dot(normed, w_query, preferred_element_type=jnp.float32), positions
    ).astype(jnp.bfloat16)
    key_rows = rotate(jnp.dot(normed, w_key, preferred_element_type=jnp.float32), positions).astype(
        jnp.bfloat16
    )
    value_rows = jnp.dot(normed, w_value, preferred_element_type=jnp.float32).astype(jnp.bfloat16)
    score_scale = 1.0 / math.sqrt(head_dim)
    run_max = jnp.full((tok_seq,), -1e30, jnp.float32)
    n_seq = lax.axis_size("seq")
    seq_index = lax.axis_index("seq")
    window = min(n_seq - 1, -(-(prompt_max - 1) // tok_seq))
    seg_rows = jnp.zeros((16, 2 * head_dim), jnp.bfloat16)
    seg_rows = seg_rows.at[0, :tok_seq].set(seg_ids.astype(jnp.bfloat16))
    packed = jnp.concatenate([jnp.concatenate([key_rows, value_rows], axis=1), seg_rows], axis=0)
    got = [packed]
    for shift in range(1, window + 1):
        pairs = [(j, j + shift) for j in range(n_seq - shift)]
        got.append(lax.ppermute(packed, "seq", pairs))
    gathered = jnp.stack(got, axis=0)
    piece_keys = gathered[:, :tok_seq, :head_dim].reshape(-1, head_dim)
    piece_values = gathered[:, :tok_seq, head_dim:].reshape(-1, head_dim)
    key_segs = gathered[:, tok_seq, :tok_seq].reshape(-1).astype(jnp.int32)
    piece_rows = piece_keys.shape[0]
    scores = (
        lax.dot_general(
            query_rows, piece_keys, (((1,), (1,)), ((), ())), preferred_element_type=jnp.float32
        )
        * score_scale
    )
    key_piece = seq_index - jnp.arange(piece_rows, dtype=jnp.int32) // tok_seq
    key_pos = key_piece * tok_seq + jnp.arange(piece_rows, dtype=jnp.int32) % tok_seq
    allowed = (
        (seg_ids[:, None] == key_segs[None, :])
        & (key_pos[None, :] <= positions[:, None])
        & (key_piece[None, :] >= 0)
    )
    masked = jnp.where(allowed, scores, -1e30)
    new_max = jnp.maximum(run_max, jnp.max(masked, axis=1))
    weights = jnp.where(allowed, jnp.exp(masked - new_max[:, None]), 0.0)
    run_total = jnp.sum(weights, axis=1)
    weighted_sum = jnp.dot(
        weights.astype(jnp.bfloat16), piece_values, preferred_element_type=jnp.float32
    )
    run_max, run_total, weighted_sum = (new_max, run_total, weighted_sum)
    head_out = (weighted_sum / run_total[:, None]).astype(jnp.bfloat16)
    partial_value = jnp.dot(head_out, w_out, preferred_element_type=jnp.float32)
    tok_dev = tok_seq // lax.axis_size("exp")
    own_start = lax.axis_index("exp") * tok_dev
    n_exp = lax.axis_size("exp")
    exp_index = lax.axis_index("exp")
    spread = lax.all_to_all(
        partial_value.reshape(n_exp, tok_dev, width), "exp", split_axis=0, concat_axis=0, tiled=True
    )
    summed = jnp.sum(spread, axis=0)
    summed = summed + lax.ppermute(summed, "section", [(0, 1), (1, 0)])
    own_rows = lax.dynamic_slice_in_dim(hidden_in, own_start, tok_dev, 0)
    residual = (own_rows.astype(jnp.float32) + summed).astype(jnp.bfloat16)
    moe_in = rms_scale(residual, moe_gain)
    experts = lax.axis_size("seq") * lax.axis_size("exp") // 2
    top_count = expert_ids.shape[1]
    capacity = min(tok_dev, max(2, 2 * tok_dev * top_count // experts))
    row_count = tok_dev * top_count
    flat_ids = expert_ids.reshape(row_count)
    one_hot = (flat_ids[:, None] == jnp.arange(experts, dtype=jnp.int32)[None, :]).astype(jnp.int32)
    slot_rank = jnp.sum((jnp.cumsum(one_hot, axis=0) - one_hot) * one_hot, axis=1)
    slot_index = flat_ids * capacity + slot_rank
    placed = slot_index[:, None] == jnp.arange(experts * capacity, dtype=jnp.int32)[None, :]
    repeated = jnp.repeat(moe_in, top_count, axis=0)
    outgoing = lax.dot_general(
        placed.astype(jnp.bfloat16),
        repeated,
        (((0,), (0,)), ((), ())),
        preferred_element_type=jnp.float32,
    ).astype(jnp.bfloat16)
    row_token = jnp.arange(row_count, dtype=jnp.int32) // top_count
    token_hot = (row_token[None, :] == jnp.arange(tok_dev, dtype=jnp.int32)[:, None]).astype(
        jnp.float32
    )
    weighted = token_hot * route_weights.reshape(row_count)[None, :]
    combine = jnp.dot(weighted, placed.astype(jnp.float32), precision=lax.Precision.HIGHEST)
    section_index = lax.axis_index("section")
    half_cap = capacity // 2
    own_half = lax.dynamic_slice_in_dim(
        outgoing.reshape(experts, capacity, width), section_index * half_cap, half_cap, 1
    )
    doubled = jnp.broadcast_to(
        own_half.reshape(experts, 1, half_cap, width), (experts, 2, half_cap, width)
    ).reshape(2 * experts, half_cap, width)
    arrived = two_stage_all_to_all(doubled)
    partner = lax.ppermute(arrived, "section", [(0, 1), (1, 0)])
    flat_rows = jnp.concatenate([arrived, partner], axis=0).reshape(-1, width)
    gate_proj = jnp.dot(flat_rows, gate_halves[0], preferred_element_type=jnp.float32)
    up_proj = jnp.dot(flat_rows, up_halves[0], preferred_element_type=jnp.float32)
    activated = (jax.nn.silu(gate_proj) * up_proj).astype(jnp.bfloat16)
    quarter_out = jnp.dot(activated, down_halves[0], preferred_element_type=jnp.float32).astype(
        jnp.bfloat16
    )
    own_rows_out = quarter_out[: arrived.shape[0] * half_cap]
    partner_rows_out = quarter_out[arrived.shape[0] * half_cap :]
    pair_sum = own_rows_out.astype(jnp.float32) + lax.ppermute(
        partner_rows_out, "section", [(0, 1), (1, 0)]
    ).astype(jnp.float32)
    returned = two_stage_all_to_all(pair_sum.astype(jnp.bfloat16).reshape(arrived.shape))
    halves_sum = jnp.sum(
        returned.reshape(experts, 2, half_cap, width).astype(jnp.float32), axis=1
    ).reshape(experts * half_cap, width)
    own_combine = lax.dynamic_slice_in_dim(
        combine.reshape(tok_dev, experts, capacity), section_index * half_cap, half_cap, 2
    ).reshape(tok_dev, experts * half_cap)
    moe_part = jnp.dot(own_combine, halves_sum, precision=lax.Precision.HIGHEST)
    moe_total = moe_part + lax.ppermute(moe_part, "section", [(0, 1), (1, 0)])
    return (residual.astype(jnp.float32) + moe_total).astype(jnp.bfloat16)


def solution(mesh):
    in_specs = (
        P("seq", None),
        P("seq"),
        P(),
        P(None, ("section", "exp")),
        P(None, ("section", "exp")),
        P(None, ("section", "exp")),
        P(("section", "exp"), None),
        P(),
        P(("seq", "exp"), None),
        P(("seq", "exp"), None),
        P(("seq", "exp"), None, "section"),
        P(("seq", "exp"), None, "section"),
        P(("seq", "exp"), "section", None),
    )
    out_specs = P(("seq", "exp"), None)
    return jax.shard_map(
        per_device, mesh=mesh, in_specs=in_specs, out_specs=out_specs, check_vma=False
    )
```

```python
import math

import jax
import jax.numpy as jnp
from jax import lax
from jax.sharding import PartitionSpec as P

epsilon = 1e-05
rope_base = 10000.0
prompt_max = 1024


def rms_scale(rows, gain):
    wide = rows.astype(jnp.float32)
    inverse = lax.rsqrt(jnp.mean(wide * wide, axis=-1, keepdims=True) + epsilon)
    return (wide * inverse * gain).astype(jnp.bfloat16)


def rotate(values, positions):
    half_dim = values.shape[-1] // 2
    frequency = rope_base ** (-2.0 * jnp.arange(half_dim, dtype=jnp.float32) / values.shape[-1])
    angles = positions.astype(jnp.float32)[:, None] * frequency[None, :]
    cosine = jnp.cos(angles)
    sine_part = jnp.sin(angles)
    first_half = values[:, :half_dim]
    second_half = values[:, half_dim:]
    return jnp.concatenate(
        [
            first_half * cosine - second_half * sine_part,
            second_half * cosine + first_half * sine_part,
        ],
        axis=-1,
    )


def per_device(
    hidden_in,
    seg_ids,
    attn_gain,
    w_query,
    w_key,
    w_value,
    w_out,
    moe_gain,
    expert_ids,
    route_weights,
    gate_halves,
    up_halves,
    down_halves,
):
    tok_seq = hidden_in.shape[0]
    width = hidden_in.shape[1]
    head_dim = w_query.shape[1]
    positions = lax.axis_index("seq") * tok_seq + jnp.arange(tok_seq, dtype=jnp.int32)
    normed = rms_scale(hidden_in, attn_gain)
    query_rows = rotate(
        jnp.dot(normed, w_query, preferred_element_type=jnp.float32), positions
    ).astype(jnp.bfloat16)
    key_rows = rotate(jnp.dot(normed, w_key, preferred_element_type=jnp.float32), positions).astype(
        jnp.bfloat16
    )
    value_rows = jnp.dot(normed, w_value, preferred_element_type=jnp.float32).astype(jnp.bfloat16)
    score_scale = 1.0 / math.sqrt(head_dim)
    run_max = jnp.full((tok_seq,), -1e30, jnp.float32)
    n_seq = lax.axis_size("seq")
    seq_index = lax.axis_index("seq")
    window = min(n_seq - 1, -(-(prompt_max - 1) // tok_seq))
    seg_rows = jnp.zeros((16, 2 * head_dim), jnp.bfloat16)
    seg_rows = seg_rows.at[0, :tok_seq].set(seg_ids.astype(jnp.bfloat16))
    packed = jnp.concatenate([jnp.concatenate([key_rows, value_rows], axis=1), seg_rows], axis=0)
    got = packed[None]
    while 2 * got.shape[0] <= window + 1:
        shift = got.shape[0]
        pairs = [(j, j + shift) for j in range(n_seq - shift)]
        got = jnp.concatenate([got, lax.ppermute(got, "seq", pairs)], axis=0)
    extra = []
    for shift in range(got.shape[0], window + 1):
        pairs = [(j, j + shift) for j in range(n_seq - shift)]
        extra.append(lax.ppermute(packed, "seq", pairs)[None])
    gathered = jnp.concatenate([got] + extra, axis=0)
    piece_keys = gathered[:, :tok_seq, :head_dim].reshape(-1, head_dim)
    piece_values = gathered[:, :tok_seq, head_dim:].reshape(-1, head_dim)
    key_segs = gathered[:, tok_seq, :tok_seq].reshape(-1).astype(jnp.int32)
    piece_rows = piece_keys.shape[0]
    scores = (
        lax.dot_general(
            query_rows, piece_keys, (((1,), (1,)), ((), ())), preferred_element_type=jnp.float32
        )
        * score_scale
    )
    key_piece = seq_index - jnp.arange(piece_rows, dtype=jnp.int32) // tok_seq
    key_pos = key_piece * tok_seq + jnp.arange(piece_rows, dtype=jnp.int32) % tok_seq
    allowed = (
        (seg_ids[:, None] == key_segs[None, :])
        & (key_pos[None, :] <= positions[:, None])
        & (key_piece[None, :] >= 0)
    )
    masked = jnp.where(allowed, scores, -1e30)
    new_max = jnp.maximum(run_max, jnp.max(masked, axis=1))
    weights = jnp.where(allowed, jnp.exp(masked - new_max[:, None]), 0.0)
    run_total = jnp.sum(weights, axis=1)
    weighted_sum = jnp.dot(
        weights.astype(jnp.bfloat16), piece_values, preferred_element_type=jnp.float32
    )
    run_max, run_total, weighted_sum = (new_max, run_total, weighted_sum)
    head_out = (weighted_sum / run_total[:, None]).astype(jnp.bfloat16)
    partial_value = jnp.dot(head_out, w_out, preferred_element_type=jnp.float32)
    tok_dev = tok_seq // lax.axis_size("exp")
    own_start = lax.axis_index("exp") * tok_dev
    n_exp = lax.axis_size("exp")
    exp_index = lax.axis_index("exp")
    summed = lax.dynamic_slice_in_dim(partial_value, own_start, tok_dev, 0)
    for shift in range(1, n_exp):
        target = (exp_index + shift) % n_exp
        chunk = lax.dynamic_slice_in_dim(partial_value, target * tok_dev, tok_dev, 0)
        pairs = [(j, (j + shift) % n_exp) for j in range(n_exp)]
        summed = summed + lax.ppermute(chunk.astype(jnp.bfloat16), "exp", pairs).astype(jnp.float32)
    summed = summed + lax.ppermute(summed, "section", [(0, 1), (1, 0)])
    own_rows = lax.dynamic_slice_in_dim(hidden_in, own_start, tok_dev, 0)
    residual = (own_rows.astype(jnp.float32) + summed).astype(jnp.bfloat16)
    moe_in = rms_scale(residual, moe_gain)
    experts = lax.axis_size("seq") * lax.axis_size("exp") // 2
    top_count = expert_ids.shape[1]
    capacity = min(tok_dev, max(2, 2 * tok_dev * top_count // experts))
    row_count = tok_dev * top_count
    flat_ids = expert_ids.reshape(row_count)
    one_hot = (flat_ids[:, None] == jnp.arange(experts, dtype=jnp.int32)[None, :]).astype(jnp.int32)
    slot_rank = jnp.sum((jnp.cumsum(one_hot, axis=0) - one_hot) * one_hot, axis=1)
    slot_index = flat_ids * capacity + slot_rank
    placed = slot_index[:, None] == jnp.arange(experts * capacity, dtype=jnp.int32)[None, :]
    repeated = jnp.repeat(moe_in, top_count, axis=0)
    outgoing = lax.dot_general(
        placed.astype(jnp.bfloat16),
        repeated,
        (((0,), (0,)), ((), ())),
        preferred_element_type=jnp.float32,
    ).astype(jnp.bfloat16)
    row_token = jnp.arange(row_count, dtype=jnp.int32) // top_count
    token_hot = (row_token[None, :] == jnp.arange(tok_dev, dtype=jnp.int32)[:, None]).astype(
        jnp.float32
    )
    weighted = token_hot * route_weights.reshape(row_count)[None, :]
    combine = jnp.dot(weighted, placed.astype(jnp.float32), precision=lax.Precision.HIGHEST)
    section_index = lax.axis_index("section")
    half_cap = capacity // 2
    own_half = lax.dynamic_slice_in_dim(
        outgoing.reshape(experts, capacity, width), section_index * half_cap, half_cap, 1
    )
    doubled = jnp.broadcast_to(
        own_half.reshape(experts, 1, half_cap, width), (experts, 2, half_cap, width)
    ).reshape(2 * experts, half_cap, width)
    arrived = lax.all_to_all(doubled, ("seq", "exp"), split_axis=0, concat_axis=0, tiled=True)
    partner = lax.ppermute(arrived, "section", [(0, 1), (1, 0)])
    flat_rows = jnp.concatenate([arrived, partner], axis=0).reshape(-1, width)
    gate_proj = jnp.dot(flat_rows, gate_halves[0], preferred_element_type=jnp.float32)
    up_proj = jnp.dot(flat_rows, up_halves[0], preferred_element_type=jnp.float32)
    activated = (jax.nn.silu(gate_proj) * up_proj).astype(jnp.bfloat16)
    quarter_out = jnp.dot(activated, down_halves[0], preferred_element_type=jnp.float32).astype(
        jnp.bfloat16
    )
    own_rows_out = quarter_out[: arrived.shape[0] * half_cap]
    partner_rows_out = quarter_out[arrived.shape[0] * half_cap :]
    pair_sum = own_rows_out.astype(jnp.float32) + lax.ppermute(
        partner_rows_out, "section", [(0, 1), (1, 0)]
    ).astype(jnp.float32)
    returned = lax.all_to_all(
        pair_sum.astype(jnp.bfloat16).reshape(arrived.shape),
        ("seq", "exp"),
        split_axis=0,
        concat_axis=0,
        tiled=True,
    )
    halves_sum = jnp.sum(
        returned.reshape(experts, 2, half_cap, width).astype(jnp.float32), axis=1
    ).reshape(experts * half_cap, width)
    own_combine = lax.dynamic_slice_in_dim(
        combine.reshape(tok_dev, experts, capacity), section_index * half_cap, half_cap, 2
    ).reshape(tok_dev, experts * half_cap)
    moe_part = jnp.dot(own_combine, halves_sum, precision=lax.Precision.HIGHEST)
    moe_total = moe_part + lax.ppermute(moe_part, "section", [(0, 1), (1, 0)])
    return (residual.astype(jnp.float32) + moe_total).astype(jnp.bfloat16)


def solution(mesh):
    in_specs = (
        P("seq", None),
        P("seq"),
        P(),
        P(None, ("section", "exp")),
        P(None, ("section", "exp")),
        P(None, ("section", "exp")),
        P(("section", "exp"), None),
        P(),
        P(("seq", "exp"), None),
        P(("seq", "exp"), None),
        P(("seq", "exp"), None, "section"),
        P(("seq", "exp"), None, "section"),
        P(("seq", "exp"), "section", None),
    )
    out_specs = P(("seq", "exp"), None)
    return jax.shard_map(
        per_device, mesh=mesh, in_specs=in_specs, out_specs=out_specs, check_vma=False
    )
```

```python
import math

import jax
import jax.numpy as jnp
from jax import lax
from jax.sharding import PartitionSpec as P

epsilon = 1e-05
rope_base = 10000.0
prompt_max = 1024


def rms_scale(rows, gain):
    wide = rows.astype(jnp.float32)
    inverse = lax.rsqrt(jnp.mean(wide * wide, axis=-1, keepdims=True) + epsilon)
    return (wide * inverse * gain).astype(jnp.bfloat16)


def rotate(values, positions):
    half_dim = values.shape[-1] // 2
    frequency = rope_base ** (-2.0 * jnp.arange(half_dim, dtype=jnp.float32) / values.shape[-1])
    angles = positions.astype(jnp.float32)[:, None] * frequency[None, :]
    cosine = jnp.cos(angles)
    sine_part = jnp.sin(angles)
    first_half = values[:, :half_dim]
    second_half = values[:, half_dim:]
    return jnp.concatenate(
        [
            first_half * cosine - second_half * sine_part,
            second_half * cosine + first_half * sine_part,
        ],
        axis=-1,
    )


def per_device(
    hidden_in,
    seg_ids,
    attn_gain,
    w_query,
    w_key,
    w_value,
    w_out,
    moe_gain,
    expert_ids,
    route_weights,
    gate_halves,
    up_halves,
    down_halves,
):
    tok_seq = hidden_in.shape[0]
    width = hidden_in.shape[1]
    head_dim = w_query.shape[1]
    positions = lax.axis_index("seq") * tok_seq + jnp.arange(tok_seq, dtype=jnp.int32)
    normed = rms_scale(hidden_in, attn_gain)
    query_rows = rotate(
        jnp.dot(normed, w_query, preferred_element_type=jnp.float32), positions
    ).astype(jnp.bfloat16)
    key_rows = rotate(jnp.dot(normed, w_key, preferred_element_type=jnp.float32), positions).astype(
        jnp.bfloat16
    )
    value_rows = jnp.dot(normed, w_value, preferred_element_type=jnp.float32).astype(jnp.bfloat16)
    score_scale = 1.0 / math.sqrt(head_dim)
    run_max = jnp.full((tok_seq,), -1e30, jnp.float32)
    n_seq = lax.axis_size("seq")
    seq_index = lax.axis_index("seq")
    window = min(n_seq - 1, -(-(prompt_max - 1) // tok_seq))
    seg_rows = jnp.zeros((16, 2 * head_dim), jnp.bfloat16)
    seg_rows = seg_rows.at[0, :tok_seq].set(seg_ids.astype(jnp.bfloat16))
    packed = jnp.concatenate([jnp.concatenate([key_rows, value_rows], axis=1), seg_rows], axis=0)
    got = [packed]
    for shift in range(1, window + 1):
        pairs = [(j, j + shift) for j in range(n_seq - shift)]
        got.append(lax.ppermute(packed, "seq", pairs))
    gathered = jnp.stack(got, axis=0)
    piece_keys = gathered[:, :tok_seq, :head_dim].reshape(-1, head_dim)
    piece_values = gathered[:, :tok_seq, head_dim:].reshape(-1, head_dim)
    key_segs = gathered[:, tok_seq, :tok_seq].reshape(-1).astype(jnp.int32)
    piece_rows = piece_keys.shape[0]
    scores = (
        lax.dot_general(
            query_rows, piece_keys, (((1,), (1,)), ((), ())), preferred_element_type=jnp.float32
        )
        * score_scale
    )
    key_piece = seq_index - jnp.arange(piece_rows, dtype=jnp.int32) // tok_seq
    key_pos = key_piece * tok_seq + jnp.arange(piece_rows, dtype=jnp.int32) % tok_seq
    allowed = (
        (seg_ids[:, None] == key_segs[None, :])
        & (key_pos[None, :] <= positions[:, None])
        & (key_piece[None, :] >= 0)
    )
    masked = jnp.where(allowed, scores, -1e30)
    new_max = jnp.maximum(run_max, jnp.max(masked, axis=1))
    weights = jnp.where(allowed, jnp.exp(masked - new_max[:, None]), 0.0)
    run_total = jnp.sum(weights, axis=1)
    weighted_sum = jnp.dot(
        weights.astype(jnp.bfloat16), piece_values, preferred_element_type=jnp.float32
    )
    run_max, run_total, weighted_sum = (new_max, run_total, weighted_sum)
    head_out = (weighted_sum / run_total[:, None]).astype(jnp.bfloat16)
    partial_value = jnp.dot(head_out, w_out, preferred_element_type=jnp.float32)
    tok_dev = tok_seq // lax.axis_size("exp")
    own_start = lax.axis_index("exp") * tok_dev
    n_exp = lax.axis_size("exp")
    exp_index = lax.axis_index("exp")
    summed = lax.dynamic_slice_in_dim(partial_value, own_start, tok_dev, 0)
    for shift in range(1, n_exp):
        target = (exp_index + shift) % n_exp
        chunk = lax.dynamic_slice_in_dim(partial_value, target * tok_dev, tok_dev, 0)
        pairs = [(j, (j + shift) % n_exp) for j in range(n_exp)]
        summed = summed + lax.ppermute(chunk.astype(jnp.bfloat16), "exp", pairs).astype(jnp.float32)
    summed = summed + lax.ppermute(summed, "section", [(0, 1), (1, 0)])
    own_rows = lax.dynamic_slice_in_dim(hidden_in, own_start, tok_dev, 0)
    residual = (own_rows.astype(jnp.float32) + summed).astype(jnp.bfloat16)
    moe_in = rms_scale(residual, moe_gain)
    experts = lax.axis_size("seq") * lax.axis_size("exp") // 2
    top_count = expert_ids.shape[1]
    capacity = min(tok_dev, max(2, 2 * tok_dev * top_count // experts))
    row_count = tok_dev * top_count
    flat_ids = expert_ids.reshape(row_count)
    one_hot = (flat_ids[:, None] == jnp.arange(experts, dtype=jnp.int32)[None, :]).astype(jnp.int32)
    slot_rank = jnp.sum((jnp.cumsum(one_hot, axis=0) - one_hot) * one_hot, axis=1)
    slot_index = flat_ids * capacity + slot_rank
    placed = slot_index[:, None] == jnp.arange(experts * capacity, dtype=jnp.int32)[None, :]
    repeated = jnp.repeat(moe_in, top_count, axis=0)
    outgoing = lax.dot_general(
        placed.astype(jnp.bfloat16),
        repeated,
        (((0,), (0,)), ((), ())),
        preferred_element_type=jnp.float32,
    ).astype(jnp.bfloat16)
    row_token = jnp.arange(row_count, dtype=jnp.int32) // top_count
    token_hot = (row_token[None, :] == jnp.arange(tok_dev, dtype=jnp.int32)[:, None]).astype(
        jnp.float32
    )
    weighted = token_hot * route_weights.reshape(row_count)[None, :]
    combine = jnp.dot(weighted, placed.astype(jnp.float32), precision=lax.Precision.HIGHEST)
    section_index = lax.axis_index("section")
    half_cap = capacity // 2
    own_half = lax.dynamic_slice_in_dim(
        outgoing.reshape(experts, capacity, width), section_index * half_cap, half_cap, 1
    )
    doubled = jnp.broadcast_to(
        own_half.reshape(experts, 1, half_cap, width), (experts, 2, half_cap, width)
    ).reshape(2 * experts, half_cap, width)
    arrived = lax.all_to_all(doubled, ("seq", "exp"), split_axis=0, concat_axis=0, tiled=True)
    partner = lax.ppermute(arrived, "section", [(0, 1), (1, 0)])
    flat_rows = jnp.concatenate([arrived, partner], axis=0).reshape(-1, width)
    gate_proj = jnp.dot(flat_rows, gate_halves[0], preferred_element_type=jnp.float32)
    up_proj = jnp.dot(flat_rows, up_halves[0], preferred_element_type=jnp.float32)
    activated = (jax.nn.silu(gate_proj) * up_proj).astype(jnp.bfloat16)
    quarter_out = jnp.dot(activated, down_halves[0], preferred_element_type=jnp.float32).astype(
        jnp.bfloat16
    )
    own_rows_out = quarter_out[: arrived.shape[0] * half_cap]
    partner_rows_out = quarter_out[arrived.shape[0] * half_cap :]
    pair_sum = own_rows_out.astype(jnp.float32) + lax.ppermute(
        partner_rows_out, "section", [(0, 1), (1, 0)]
    ).astype(jnp.float32)
    returned = lax.all_to_all(
        pair_sum.astype(jnp.bfloat16).reshape(arrived.shape),
        ("seq", "exp"),
        split_axis=0,
        concat_axis=0,
        tiled=True,
    )
    halves_sum = jnp.sum(
        returned.reshape(experts, 2, half_cap, width).astype(jnp.float32), axis=1
    ).reshape(experts * half_cap, width)
    own_combine = lax.dynamic_slice_in_dim(
        combine.reshape(tok_dev, experts, capacity), section_index * half_cap, half_cap, 2
    ).reshape(tok_dev, experts * half_cap)
    moe_part = jnp.dot(own_combine, halves_sum, precision=lax.Precision.HIGHEST)
    moe_total = moe_part + lax.ppermute(moe_part, "section", [(0, 1), (1, 0)])
    return (residual.astype(jnp.float32) + moe_total).astype(jnp.bfloat16)


def solution(mesh):
    in_specs = (
        P("seq", None),
        P("seq"),
        P(),
        P(None, ("section", "exp")),
        P(None, ("section", "exp")),
        P(None, ("section", "exp")),
        P(("section", "exp"), None),
        P(),
        P(("seq", "exp"), None),
        P(("seq", "exp"), None),
        P(("seq", "exp"), None, "section"),
        P(("seq", "exp"), None, "section"),
        P(("seq", "exp"), "section", None),
    )
    out_specs = P(("seq", "exp"), None)
    return jax.shard_map(
        per_device, mesh=mesh, in_specs=in_specs, out_specs=out_specs, check_vma=False
    )
```

```python
import math

import jax
import jax.numpy as jnp
from jax import lax
from jax.sharding import PartitionSpec as P

epsilon = 1e-05
rope_base = 10000.0
prompt_max = 1024


def rms_scale(rows, gain):
    wide = rows.astype(jnp.float32)
    inverse = lax.rsqrt(jnp.mean(wide * wide, axis=-1, keepdims=True) + epsilon)
    return (wide * inverse * gain).astype(jnp.bfloat16)


def rotate(values, positions):
    half_dim = values.shape[-1] // 2
    frequency = rope_base ** (-2.0 * jnp.arange(half_dim, dtype=jnp.float32) / values.shape[-1])
    angles = positions.astype(jnp.float32)[:, None] * frequency[None, :]
    cosine = jnp.cos(angles)
    sine_part = jnp.sin(angles)
    first_half = values[:, :half_dim]
    second_half = values[:, half_dim:]
    return jnp.concatenate(
        [
            first_half * cosine - second_half * sine_part,
            second_half * cosine + first_half * sine_part,
        ],
        axis=-1,
    )


def per_device(
    hidden_in,
    seg_ids,
    attn_gain,
    w_query,
    w_key,
    w_value,
    w_out,
    moe_gain,
    expert_ids,
    route_weights,
    gate_halves,
    up_halves,
    down_halves,
):
    tok_seq = hidden_in.shape[0]
    width = hidden_in.shape[1]
    head_dim = w_query.shape[1]
    positions = lax.axis_index("seq") * tok_seq + jnp.arange(tok_seq, dtype=jnp.int32)
    normed = rms_scale(hidden_in, attn_gain)
    query_rows = rotate(
        jnp.dot(normed, w_query, preferred_element_type=jnp.float32), positions
    ).astype(jnp.bfloat16)
    key_rows = rotate(jnp.dot(normed, w_key, preferred_element_type=jnp.float32), positions).astype(
        jnp.bfloat16
    )
    value_rows = jnp.dot(normed, w_value, preferred_element_type=jnp.float32).astype(jnp.bfloat16)
    score_scale = 1.0 / math.sqrt(head_dim)
    n_seq = lax.axis_size("seq")
    seq_index = lax.axis_index("seq")
    window = min(n_seq - 1, -(-(prompt_max - 1) // tok_seq))
    seg_rows = jnp.zeros((16, 2 * head_dim), jnp.bfloat16)
    seg_rows = seg_rows.at[0, :tok_seq].set(seg_ids.astype(jnp.bfloat16))
    packed = jnp.concatenate([jnp.concatenate([key_rows, value_rows], axis=1), seg_rows], axis=0)
    got = [packed]
    for shift in range(1, window + 1):
        pairs = [(j, j + shift) for j in range(n_seq - shift)]
        got.append(lax.ppermute(packed, "seq", pairs))
    masked_list = []
    allowed_list = []
    for shift, block in enumerate(got):
        piece_keys = block[:tok_seq, :head_dim]
        key_segs = block[tok_seq, :tok_seq].astype(jnp.int32)
        scores = (
            lax.dot_general(
                query_rows, piece_keys, (((1,), (1,)), ((), ())), preferred_element_type=jnp.float32
            )
            * score_scale
        )
        key_piece = seq_index - shift
        key_pos = key_piece * tok_seq + jnp.arange(tok_seq, dtype=jnp.int32)
        allowed = (
            (seg_ids[:, None] == key_segs[None, :])
            & (key_pos[None, :] <= positions[:, None])
            & (key_piece >= 0)
        )
        masked_list.append(jnp.where(allowed, scores, -1e30))
        allowed_list.append(allowed)
    run_max = jnp.max(jnp.stack([jnp.max(m, axis=1) for m in masked_list], axis=0), axis=0)
    run_total = jnp.zeros((tok_seq,), jnp.float32)
    weighted_sum = jnp.zeros((tok_seq, head_dim), jnp.float32)
    for block, masked, allowed in zip(got, masked_list, allowed_list):
        weights = jnp.where(allowed, jnp.exp(masked - run_max[:, None]), 0.0)
        run_total = run_total + jnp.sum(weights, axis=1)
        weighted_sum = weighted_sum + jnp.dot(
            weights.astype(jnp.bfloat16), block[:tok_seq, head_dim:], preferred_element_type=jnp.float32
        )
    head_out = (weighted_sum / run_total[:, None]).astype(jnp.bfloat16)
    partial_value = jnp.dot(head_out, w_out, preferred_element_type=jnp.float32)
    tok_dev = tok_seq // lax.axis_size("exp")
    own_start = lax.axis_index("exp") * tok_dev
    n_exp = lax.axis_size("exp")
    exp_index = lax.axis_index("exp")
    summed = lax.dynamic_slice_in_dim(partial_value, own_start, tok_dev, 0)
    for shift in range(1, n_exp):
        target = (exp_index + shift) % n_exp
        chunk = lax.dynamic_slice_in_dim(partial_value, target * tok_dev, tok_dev, 0)
        pairs = [(j, (j + shift) % n_exp) for j in range(n_exp)]
        summed = summed + lax.ppermute(chunk.astype(jnp.bfloat16), "exp", pairs).astype(jnp.float32)
    summed = summed + lax.ppermute(summed, "section", [(0, 1), (1, 0)])
    own_rows = lax.dynamic_slice_in_dim(hidden_in, own_start, tok_dev, 0)
    residual = (own_rows.astype(jnp.float32) + summed).astype(jnp.bfloat16)
    moe_in = rms_scale(residual, moe_gain)
    experts = lax.axis_size("seq") * lax.axis_size("exp") // 2
    top_count = expert_ids.shape[1]
    capacity = min(tok_dev, max(2, 2 * tok_dev * top_count // experts))
    row_count = tok_dev * top_count
    flat_ids = expert_ids.reshape(row_count)
    one_hot = (flat_ids[:, None] == jnp.arange(experts, dtype=jnp.int32)[None, :]).astype(jnp.int32)
    slot_rank = jnp.sum((jnp.cumsum(one_hot, axis=0) - one_hot) * one_hot, axis=1)
    slot_index = flat_ids * capacity + slot_rank
    placed = slot_index[:, None] == jnp.arange(experts * capacity, dtype=jnp.int32)[None, :]
    repeated = jnp.repeat(moe_in, top_count, axis=0)
    outgoing = lax.dot_general(
        placed.astype(jnp.bfloat16),
        repeated,
        (((0,), (0,)), ((), ())),
        preferred_element_type=jnp.float32,
    ).astype(jnp.bfloat16)
    row_token = jnp.arange(row_count, dtype=jnp.int32) // top_count
    token_hot = (row_token[None, :] == jnp.arange(tok_dev, dtype=jnp.int32)[:, None]).astype(
        jnp.float32
    )
    weighted = token_hot * route_weights.reshape(row_count)[None, :]
    combine = jnp.dot(weighted, placed.astype(jnp.float32), precision=lax.Precision.HIGHEST)
    section_index = lax.axis_index("section")
    half_cap = capacity // 2
    own_half = lax.dynamic_slice_in_dim(
        outgoing.reshape(experts, capacity, width), section_index * half_cap, half_cap, 1
    )
    doubled = jnp.broadcast_to(
        own_half.reshape(experts, 1, half_cap, width), (experts, 2, half_cap, width)
    ).reshape(2 * experts, half_cap, width)
    arrived = lax.all_to_all(doubled, ("seq", "exp"), split_axis=0, concat_axis=0, tiled=True)
    partner = lax.ppermute(arrived, "section", [(0, 1), (1, 0)])

    def quarter_ffn(rows):
        gate_proj = jnp.dot(rows, gate_halves[0], preferred_element_type=jnp.float32)
        up_proj = jnp.dot(rows, up_halves[0], preferred_element_type=jnp.float32)
        activated = (jax.nn.silu(gate_proj) * up_proj).astype(jnp.bfloat16)
        return jnp.dot(activated, down_halves[0], preferred_element_type=jnp.float32).astype(
            jnp.bfloat16
        )

    own_rows_out = quarter_ffn(arrived.reshape(-1, width))
    partner_rows_out = quarter_ffn(partner.reshape(-1, width))
    pair_sum = own_rows_out.astype(jnp.float32) + lax.ppermute(
        partner_rows_out, "section", [(0, 1), (1, 0)]
    ).astype(jnp.float32)
    returned = lax.all_to_all(
        pair_sum.astype(jnp.bfloat16).reshape(arrived.shape),
        ("seq", "exp"),
        split_axis=0,
        concat_axis=0,
        tiled=True,
    )
    halves_sum = jnp.sum(
        returned.reshape(experts, 2, half_cap, width).astype(jnp.float32), axis=1
    ).reshape(experts * half_cap, width)
    own_combine = lax.dynamic_slice_in_dim(
        combine.reshape(tok_dev, experts, capacity), section_index * half_cap, half_cap, 2
    ).reshape(tok_dev, experts * half_cap)
    moe_part = jnp.dot(own_combine, halves_sum, precision=lax.Precision.HIGHEST)
    moe_total = moe_part + lax.ppermute(moe_part, "section", [(0, 1), (1, 0)])
    return (residual.astype(jnp.float32) + moe_total).astype(jnp.bfloat16)


def solution(mesh):
    in_specs = (
        P("seq", None),
        P("seq"),
        P(),
        P(None, ("section", "exp")),
        P(None, ("section", "exp")),
        P(None, ("section", "exp")),
        P(("section", "exp"), None),
        P(),
        P(("seq", "exp"), None),
        P(("seq", "exp"), None),
        P(("seq", "exp"), None, "section"),
        P(("seq", "exp"), None, "section"),
        P(("seq", "exp"), "section", None),
    )
    out_specs = P(("seq", "exp"), None)
    return jax.shard_map(
        per_device, mesh=mesh, in_specs=in_specs, out_specs=out_specs, check_vma=False
    )
```

```python
import math

import jax
import jax.numpy as jnp
from jax import lax
from jax.sharding import PartitionSpec as P

epsilon = 1e-05
rope_base = 10000.0
prompt_max = 1024


def rms_scale(rows, gain):
    wide = rows.astype(jnp.float32)
    inverse = lax.rsqrt(jnp.mean(wide * wide, axis=-1, keepdims=True) + epsilon)
    return (wide * inverse * gain).astype(jnp.bfloat16)


def rotate(values, positions):
    half_dim = values.shape[-1] // 2
    frequency = rope_base ** (-2.0 * jnp.arange(half_dim, dtype=jnp.float32) / values.shape[-1])
    angles = positions.astype(jnp.float32)[:, None] * frequency[None, :]
    cosine = jnp.cos(angles)
    sine_part = jnp.sin(angles)
    first_half = values[:, :half_dim]
    second_half = values[:, half_dim:]
    return jnp.concatenate(
        [
            first_half * cosine - second_half * sine_part,
            second_half * cosine + first_half * sine_part,
        ],
        axis=-1,
    )


def per_device(
    hidden_in,
    seg_ids,
    attn_gain,
    w_query,
    w_key,
    w_value,
    w_out,
    moe_gain,
    expert_ids,
    route_weights,
    gate_halves,
    up_halves,
    down_halves,
):
    tok_seq = hidden_in.shape[0]
    width = hidden_in.shape[1]
    head_dim = w_query.shape[1]
    positions = lax.axis_index("seq") * tok_seq + jnp.arange(tok_seq, dtype=jnp.int32)
    normed = rms_scale(hidden_in, attn_gain)
    query_rows = rotate(
        jnp.dot(normed, w_query, preferred_element_type=jnp.float32), positions
    ).astype(jnp.bfloat16)
    key_rows = rotate(jnp.dot(normed, w_key, preferred_element_type=jnp.float32), positions).astype(
        jnp.bfloat16
    )
    value_rows = jnp.dot(normed, w_value, preferred_element_type=jnp.float32).astype(jnp.bfloat16)
    score_scale = 1.0 / math.sqrt(head_dim)
    n_seq = lax.axis_size("seq")
    seq_index = lax.axis_index("seq")
    window = min(n_seq - 1, -(-(prompt_max - 1) // tok_seq))
    seg_rows = jnp.zeros((16, 2 * head_dim), jnp.bfloat16)
    seg_rows = seg_rows.at[0, :tok_seq].set(seg_ids.astype(jnp.bfloat16))
    packed = jnp.concatenate([jnp.concatenate([key_rows, value_rows], axis=1), seg_rows], axis=0)
    section_index = lax.axis_index("section")
    swap = [(0, 1), (1, 0)]
    other_head = lax.ppermute(packed, "section", swap)
    both_heads = jnp.where(
        section_index == 0, jnp.stack([packed, other_head]), jnp.stack([other_head, packed])
    )
    steps = -(-window // 2)
    own_got = []
    kept = []
    for step in range(steps):
        pairs = []
        for core in range(2):
            shift = 2 * step + 1 + core
            if shift <= window:
                pairs += [(core * n_seq + j, core * n_seq + j + shift) for j in range(n_seq - shift)]
        arrived_pair = lax.ppermute(both_heads, ("section", "seq"), pairs)
        own_got.append(lax.dynamic_index_in_dim(arrived_pair, section_index, 0, keepdims=False))
        kept.append(lax.dynamic_index_in_dim(arrived_pair, 1 - section_index, 0, keepdims=False))
    from_partner = lax.ppermute(jnp.stack(kept), "section", swap)
    got = [packed]
    for step in range(steps):
        odd_block = jnp.where(section_index == 0, own_got[step], from_partner[step])
        even_block = jnp.where(section_index == 0, from_partner[step], own_got[step])
        got.append(odd_block)
        if 2 * step + 2 <= window:
            got.append(even_block)
    masked_list = []
    allowed_list = []
    for shift, block in enumerate(got):
        piece_keys = block[:tok_seq, :head_dim]
        key_segs = block[tok_seq, :tok_seq].astype(jnp.int32)
        scores = (
            lax.dot_general(
                query_rows, piece_keys, (((1,), (1,)), ((), ())), preferred_element_type=jnp.float32
            )
            * score_scale
        )
        key_piece = seq_index - shift
        key_pos = key_piece * tok_seq + jnp.arange(tok_seq, dtype=jnp.int32)
        allowed = (
            (seg_ids[:, None] == key_segs[None, :])
            & (key_pos[None, :] <= positions[:, None])
            & (key_piece >= 0)
        )
        masked_list.append(jnp.where(allowed, scores, -1e30))
        allowed_list.append(allowed)
    run_max = jnp.max(jnp.stack([jnp.max(m, axis=1) for m in masked_list], axis=0), axis=0)
    run_total = jnp.zeros((tok_seq,), jnp.float32)
    weighted_sum = jnp.zeros((tok_seq, head_dim), jnp.float32)
    for block, masked, allowed in zip(got, masked_list, allowed_list):
        weights = jnp.where(allowed, jnp.exp(masked - run_max[:, None]), 0.0)
        run_total = run_total + jnp.sum(weights, axis=1)
        weighted_sum = weighted_sum + jnp.dot(
            weights.astype(jnp.bfloat16), block[:tok_seq, head_dim:], preferred_element_type=jnp.float32
        )
    head_out = (weighted_sum / run_total[:, None]).astype(jnp.bfloat16)
    partial_value = jnp.dot(head_out, w_out, preferred_element_type=jnp.float32)
    tok_dev = tok_seq // lax.axis_size("exp")
    own_start = lax.axis_index("exp") * tok_dev
    n_exp = lax.axis_size("exp")
    exp_index = lax.axis_index("exp")
    section_sum = partial_value + lax.ppermute(partial_value, "section", swap)
    summed = jnp.where(
        section_index == 0,
        lax.dynamic_slice_in_dim(section_sum, own_start, tok_dev, 0),
        jnp.zeros((tok_dev, width), jnp.float32),
    )
    for step in range(n_exp // 2):
        pairs = []
        for core in range(2):
            shift = 2 * step + 1 + core
            if shift < n_exp:
                pairs += [(core * n_exp + j, core * n_exp + (j + shift) % n_exp) for j in range(n_exp)]
        target = (exp_index + 2 * step + 1 + section_index) % n_exp
        chunk = lax.dynamic_slice_in_dim(section_sum, target * tok_dev, tok_dev, 0)
        summed = summed + lax.ppermute(
            chunk.astype(jnp.bfloat16), ("section", "exp"), pairs
        ).astype(jnp.float32)
    summed = summed + lax.ppermute(summed, "section", swap)
    own_rows = lax.dynamic_slice_in_dim(hidden_in, own_start, tok_dev, 0)
    residual = (own_rows.astype(jnp.float32) + summed).astype(jnp.bfloat16)
    moe_in = rms_scale(residual, moe_gain)
    experts = lax.axis_size("seq") * lax.axis_size("exp") // 2
    top_count = expert_ids.shape[1]
    capacity = min(tok_dev, max(2, 2 * tok_dev * top_count // experts))
    row_count = tok_dev * top_count
    flat_ids = expert_ids.reshape(row_count)
    one_hot = (flat_ids[:, None] == jnp.arange(experts, dtype=jnp.int32)[None, :]).astype(jnp.int32)
    slot_rank = jnp.sum((jnp.cumsum(one_hot, axis=0) - one_hot) * one_hot, axis=1)
    slot_index = flat_ids * capacity + slot_rank
    placed = slot_index[:, None] == jnp.arange(experts * capacity, dtype=jnp.int32)[None, :]
    repeated = jnp.repeat(moe_in, top_count, axis=0)
    outgoing = lax.dot_general(
        placed.astype(jnp.bfloat16),
        repeated,
        (((0,), (0,)), ((), ())),
        preferred_element_type=jnp.float32,
    ).astype(jnp.bfloat16)
    row_token = jnp.arange(row_count, dtype=jnp.int32) // top_count
    token_hot = (row_token[None, :] == jnp.arange(tok_dev, dtype=jnp.int32)[:, None]).astype(
        jnp.float32
    )
    weighted = token_hot * route_weights.reshape(row_count)[None, :]
    combine = jnp.dot(weighted, placed.astype(jnp.float32), precision=lax.Precision.HIGHEST)
    half_cap = capacity // 2
    own_half = lax.dynamic_slice_in_dim(
        outgoing.reshape(experts, capacity, width), section_index * half_cap, half_cap, 1
    )
    doubled = jnp.broadcast_to(
        own_half.reshape(experts, 1, half_cap, width), (experts, 2, half_cap, width)
    ).reshape(2 * experts, half_cap, width)
    arrived = lax.all_to_all(doubled, ("seq", "exp"), split_axis=0, concat_axis=0, tiled=True)
    partner = lax.ppermute(arrived, "section", [(0, 1), (1, 0)])

    def quarter_ffn(rows):
        gate_proj = jnp.dot(rows, gate_halves[0], preferred_element_type=jnp.float32)
        up_proj = jnp.dot(rows, up_halves[0], preferred_element_type=jnp.float32)
        activated = (jax.nn.silu(gate_proj) * up_proj).astype(jnp.bfloat16)
        return jnp.dot(activated, down_halves[0], preferred_element_type=jnp.float32).astype(
            jnp.bfloat16
        )

    own_rows_out = quarter_ffn(arrived.reshape(-1, width))
    partner_rows_out = quarter_ffn(partner.reshape(-1, width))
    pair_sum = own_rows_out.astype(jnp.float32) + lax.ppermute(
        partner_rows_out, "section", [(0, 1), (1, 0)]
    ).astype(jnp.float32)
    returned = lax.all_to_all(
        pair_sum.astype(jnp.bfloat16).reshape(arrived.shape),
        ("seq", "exp"),
        split_axis=0,
        concat_axis=0,
        tiled=True,
    )
    halves_sum = jnp.sum(
        returned.reshape(experts, 2, half_cap, width).astype(jnp.float32), axis=1
    ).reshape(experts * half_cap, width)
    own_combine = lax.dynamic_slice_in_dim(
        combine.reshape(tok_dev, experts, capacity), section_index * half_cap, half_cap, 2
    ).reshape(tok_dev, experts * half_cap)
    moe_part = jnp.dot(own_combine, halves_sum, precision=lax.Precision.HIGHEST)
    moe_total = moe_part + lax.ppermute(moe_part, "section", [(0, 1), (1, 0)])
    return (residual.astype(jnp.float32) + moe_total).astype(jnp.bfloat16)


def solution(mesh):
    in_specs = (
        P("seq", None),
        P("seq"),
        P(),
        P(None, ("section", "exp")),
        P(None, ("section", "exp")),
        P(None, ("section", "exp")),
        P(("section", "exp"), None),
        P(),
        P(("seq", "exp"), None),
        P(("seq", "exp"), None),
        P(("seq", "exp"), None, "section"),
        P(("seq", "exp"), None, "section"),
        P(("seq", "exp"), "section", None),
    )
    out_specs = P(("seq", "exp"), None)
    return jax.shard_map(
        per_device, mesh=mesh, in_specs=in_specs, out_specs=out_specs, check_vma=False
    )
```

```python
import math

import jax
import jax.numpy as jnp
from jax import lax
from jax.sharding import PartitionSpec as P

epsilon = 1e-05
rope_base = 10000.0
prompt_max = 1024


def rms_scale(rows, gain):
    wide = rows.astype(jnp.float32)
    inverse = lax.rsqrt(jnp.mean(wide * wide, axis=-1, keepdims=True) + epsilon)
    return (wide * inverse * gain).astype(jnp.bfloat16)


def rotate(values, positions):
    half_dim = values.shape[-1] // 2
    frequency = rope_base ** (-2.0 * jnp.arange(half_dim, dtype=jnp.float32) / values.shape[-1])
    angles = positions.astype(jnp.float32)[:, None] * frequency[None, :]
    cosine = jnp.cos(angles)
    sine_part = jnp.sin(angles)
    first_half = values[:, :half_dim]
    second_half = values[:, half_dim:]
    return jnp.concatenate(
        [
            first_half * cosine - second_half * sine_part,
            second_half * cosine + first_half * sine_part,
        ],
        axis=-1,
    )


def per_device(
    hidden_in,
    seg_ids,
    attn_gain,
    w_query,
    w_key,
    w_value,
    w_out,
    moe_gain,
    expert_ids,
    route_weights,
    gate_halves,
    up_halves,
    down_halves,
):
    tok_seq = hidden_in.shape[0]
    width = hidden_in.shape[1]
    head_dim = w_query.shape[1]
    positions = lax.axis_index("seq") * tok_seq + jnp.arange(tok_seq, dtype=jnp.int32)
    normed = rms_scale(hidden_in, attn_gain)
    query_rows = rotate(
        jnp.dot(normed, w_query, preferred_element_type=jnp.float32), positions
    ).astype(jnp.bfloat16)
    key_rows = rotate(jnp.dot(normed, w_key, preferred_element_type=jnp.float32), positions).astype(
        jnp.bfloat16
    )
    value_rows = jnp.dot(normed, w_value, preferred_element_type=jnp.float32).astype(jnp.bfloat16)
    score_scale = 1.0 / math.sqrt(head_dim)
    n_seq = lax.axis_size("seq")
    seq_index = lax.axis_index("seq")
    window = min(n_seq - 1, -(-(prompt_max - 1) // tok_seq))
    seg_rows = jnp.zeros((16, 2 * head_dim), jnp.bfloat16)
    seg_rows = seg_rows.at[0, :tok_seq].set(seg_ids.astype(jnp.bfloat16))
    packed = jnp.concatenate([jnp.concatenate([key_rows, value_rows], axis=1), seg_rows], axis=0)
    section_index = lax.axis_index("section")
    swap = [(0, 1), (1, 0)]
    got = [packed]
    for shift in range(1, window + 1):
        pairs = [(j, j + shift) for j in range(n_seq - shift)]
        got.append(lax.ppermute(packed, "seq", pairs))
    masked_list = []
    allowed_list = []
    for shift, block in enumerate(got):
        piece_keys = block[:tok_seq, :head_dim]
        key_segs = block[tok_seq, :tok_seq].astype(jnp.int32)
        scores = (
            lax.dot_general(
                query_rows, piece_keys, (((1,), (1,)), ((), ())), preferred_element_type=jnp.float32
            )
            * score_scale
        )
        key_piece = seq_index - shift
        key_pos = key_piece * tok_seq + jnp.arange(tok_seq, dtype=jnp.int32)
        allowed = (
            (seg_ids[:, None] == key_segs[None, :])
            & (key_pos[None, :] <= positions[:, None])
            & (key_piece >= 0)
        )
        masked_list.append(jnp.where(allowed, scores, -1e30))
        allowed_list.append(allowed)
    run_max = jnp.max(jnp.stack([jnp.max(m, axis=1) for m in masked_list], axis=0), axis=0)
    run_total = jnp.zeros((tok_seq,), jnp.float32)
    weighted_sum = jnp.zeros((tok_seq, head_dim), jnp.float32)
    for block, masked, allowed in zip(got, masked_list, allowed_list):
        weights = jnp.where(allowed, jnp.exp(masked - run_max[:, None]), 0.0)
        run_total = run_total + jnp.sum(weights, axis=1)
        weighted_sum = weighted_sum + jnp.dot(
            weights.astype(jnp.bfloat16), block[:tok_seq, head_dim:], preferred_element_type=jnp.float32
        )
    head_out = (weighted_sum / run_total[:, None]).astype(jnp.bfloat16)
    partial_value = jnp.dot(head_out, w_out, preferred_element_type=jnp.float32)
    tok_dev = tok_seq // lax.axis_size("exp")
    own_start = lax.axis_index("exp") * tok_dev
    n_exp = lax.axis_size("exp")
    exp_index = lax.axis_index("exp")
    section_sum = partial_value + lax.ppermute(partial_value, "section", swap)
    summed = jnp.where(
        section_index == 0,
        lax.dynamic_slice_in_dim(section_sum, own_start, tok_dev, 0),
        jnp.zeros((tok_dev, width), jnp.float32),
    )
    for step in range(n_exp // 2):
        pairs = []
        for core in range(2):
            shift = 2 * step + 1 + core
            if shift < n_exp:
                pairs += [(core * n_exp + j, core * n_exp + (j + shift) % n_exp) for j in range(n_exp)]
        target = (exp_index + 2 * step + 1 + section_index) % n_exp
        chunk = lax.dynamic_slice_in_dim(section_sum, target * tok_dev, tok_dev, 0)
        summed = summed + lax.ppermute(
            chunk.astype(jnp.bfloat16), ("section", "exp"), pairs
        ).astype(jnp.float32)
    summed = summed + lax.ppermute(summed, "section", swap)
    own_rows = lax.dynamic_slice_in_dim(hidden_in, own_start, tok_dev, 0)
    residual = (own_rows.astype(jnp.float32) + summed).astype(jnp.bfloat16)
    moe_in = rms_scale(residual, moe_gain)
    experts = lax.axis_size("seq") * lax.axis_size("exp") // 2
    top_count = expert_ids.shape[1]
    capacity = min(tok_dev, max(2, 2 * tok_dev * top_count // experts))
    row_count = tok_dev * top_count
    flat_ids = expert_ids.reshape(row_count)
    one_hot = (flat_ids[:, None] == jnp.arange(experts, dtype=jnp.int32)[None, :]).astype(jnp.int32)
    slot_rank = jnp.sum((jnp.cumsum(one_hot, axis=0) - one_hot) * one_hot, axis=1)
    slot_index = flat_ids * capacity + slot_rank
    placed = slot_index[:, None] == jnp.arange(experts * capacity, dtype=jnp.int32)[None, :]
    repeated = jnp.repeat(moe_in, top_count, axis=0)
    outgoing = lax.dot_general(
        placed.astype(jnp.bfloat16),
        repeated,
        (((0,), (0,)), ((), ())),
        preferred_element_type=jnp.float32,
    ).astype(jnp.bfloat16)
    row_token = jnp.arange(row_count, dtype=jnp.int32) // top_count
    token_hot = (row_token[None, :] == jnp.arange(tok_dev, dtype=jnp.int32)[:, None]).astype(
        jnp.float32
    )
    weighted = token_hot * route_weights.reshape(row_count)[None, :]
    combine = jnp.dot(weighted, placed.astype(jnp.float32), precision=lax.Precision.HIGHEST)
    half_cap = capacity // 2
    own_half = lax.dynamic_slice_in_dim(
        outgoing.reshape(experts, capacity, width), section_index * half_cap, half_cap, 1
    )
    doubled = jnp.broadcast_to(
        own_half.reshape(experts, 1, half_cap, width), (experts, 2, half_cap, width)
    ).reshape(2 * experts, half_cap, width)
    arrived = lax.all_to_all(doubled, ("seq", "exp"), split_axis=0, concat_axis=0, tiled=True)
    partner = lax.ppermute(arrived, "section", [(0, 1), (1, 0)])

    def quarter_ffn(rows):
        gate_proj = jnp.dot(rows, gate_halves[0], preferred_element_type=jnp.float32)
        up_proj = jnp.dot(rows, up_halves[0], preferred_element_type=jnp.float32)
        activated = (jax.nn.silu(gate_proj) * up_proj).astype(jnp.bfloat16)
        return jnp.dot(activated, down_halves[0], preferred_element_type=jnp.float32).astype(
            jnp.bfloat16
        )

    own_rows_out = quarter_ffn(arrived.reshape(-1, width))
    partner_rows_out = quarter_ffn(partner.reshape(-1, width))
    pair_sum = own_rows_out.astype(jnp.float32) + lax.ppermute(
        partner_rows_out, "section", [(0, 1), (1, 0)]
    ).astype(jnp.float32)
    returned = lax.all_to_all(
        pair_sum.astype(jnp.bfloat16).reshape(arrived.shape),
        ("seq", "exp"),
        split_axis=0,
        concat_axis=0,
        tiled=True,
    )
    halves_sum = jnp.sum(
        returned.reshape(experts, 2, half_cap, width).astype(jnp.float32), axis=1
    ).reshape(experts * half_cap, width)
    own_combine = lax.dynamic_slice_in_dim(
        combine.reshape(tok_dev, experts, capacity), section_index * half_cap, half_cap, 2
    ).reshape(tok_dev, experts * half_cap)
    moe_part = jnp.dot(own_combine, halves_sum, precision=lax.Precision.HIGHEST)
    moe_total = moe_part + lax.ppermute(moe_part, "section", [(0, 1), (1, 0)])
    return (residual.astype(jnp.float32) + moe_total).astype(jnp.bfloat16)


def solution(mesh):
    in_specs = (
        P("seq", None),
        P("seq"),
        P(),
        P(None, ("section", "exp")),
        P(None, ("section", "exp")),
        P(None, ("section", "exp")),
        P(("section", "exp"), None),
        P(),
        P(("seq", "exp"), None),
        P(("seq", "exp"), None),
        P(("seq", "exp"), None, "section"),
        P(("seq", "exp"), None, "section"),
        P(("seq", "exp"), "section", None),
    )
    out_specs = P(("seq", "exp"), None)
    return jax.shard_map(
        per_device, mesh=mesh, in_specs=in_specs, out_specs=out_specs, check_vma=False
    )
```

```python
import math

import jax
import jax.numpy as jnp
from jax import lax
from jax.sharding import PartitionSpec as P

epsilon = 1e-05
rope_base = 10000.0
prompt_max = 1024


def rms_scale(rows, gain):
    wide = rows.astype(jnp.float32)
    inverse = lax.rsqrt(jnp.mean(wide * wide, axis=-1, keepdims=True) + epsilon)
    return (wide * inverse * gain).astype(jnp.bfloat16)


def rotate(values, positions):
    half_dim = values.shape[-1] // 2
    frequency = rope_base ** (-2.0 * jnp.arange(half_dim, dtype=jnp.float32) / values.shape[-1])
    angles = positions.astype(jnp.float32)[:, None] * frequency[None, :]
    cosine = jnp.cos(angles)
    sine_part = jnp.sin(angles)
    first_half = values[:, :half_dim]
    second_half = values[:, half_dim:]
    return jnp.concatenate(
        [
            first_half * cosine - second_half * sine_part,
            second_half * cosine + first_half * sine_part,
        ],
        axis=-1,
    )


def per_device(
    hidden_in,
    seg_ids,
    attn_gain,
    w_query,
    w_key,
    w_value,
    w_out,
    moe_gain,
    expert_ids,
    route_weights,
    gate_halves,
    up_halves,
    down_halves,
):
    tok_seq = hidden_in.shape[0]
    width = hidden_in.shape[1]
    head_dim = w_query.shape[1]
    positions = lax.axis_index("seq") * tok_seq + jnp.arange(tok_seq, dtype=jnp.int32)
    normed = rms_scale(hidden_in, attn_gain)
    query_rows = rotate(
        jnp.dot(normed, w_query, preferred_element_type=jnp.float32), positions
    ).astype(jnp.bfloat16)
    key_rows = rotate(jnp.dot(normed, w_key, preferred_element_type=jnp.float32), positions).astype(
        jnp.bfloat16
    )
    value_rows = jnp.dot(normed, w_value, preferred_element_type=jnp.float32).astype(jnp.bfloat16)
    score_scale = 1.0 / math.sqrt(head_dim)
    n_seq = lax.axis_size("seq")
    seq_index = lax.axis_index("seq")
    window = min(n_seq - 1, -(-(prompt_max - 1) // tok_seq))
    seg_rows = jnp.zeros((16, 2 * head_dim), jnp.bfloat16)
    seg_rows = seg_rows.at[0, :tok_seq].set(seg_ids.astype(jnp.bfloat16))
    packed = jnp.concatenate([jnp.concatenate([key_rows, value_rows], axis=1), seg_rows], axis=0)
    section_index = lax.axis_index("section")
    swap = [(0, 1), (1, 0)]
    first = -(-window // 2)
    got = [packed]
    for shift in range(1, first + 1):
        pairs = [(j, j + shift) for j in range(n_seq - shift)]
        got.append(lax.ppermute(packed, "seq", pairs))
    if window > first:
        pairs = [(j, j + first) for j in range(n_seq - first)]
        relayed = lax.ppermute(jnp.stack(got[1 : window - first + 1]), "seq", pairs)
        got += [relayed[k] for k in range(window - first)]
    masked_list = []
    allowed_list = []
    for shift, block in enumerate(got):
        piece_keys = block[:tok_seq, :head_dim]
        key_segs = block[tok_seq, :tok_seq].astype(jnp.int32)
        scores = (
            lax.dot_general(
                query_rows, piece_keys, (((1,), (1,)), ((), ())), preferred_element_type=jnp.float32
            )
            * score_scale
        )
        key_piece = seq_index - shift
        key_pos = key_piece * tok_seq + jnp.arange(tok_seq, dtype=jnp.int32)
        allowed = (
            (seg_ids[:, None] == key_segs[None, :])
            & (key_pos[None, :] <= positions[:, None])
            & (key_piece >= 0)
        )
        masked_list.append(jnp.where(allowed, scores, -1e30))
        allowed_list.append(allowed)
    run_max = jnp.max(jnp.stack([jnp.max(m, axis=1) for m in masked_list], axis=0), axis=0)
    run_total = jnp.zeros((tok_seq,), jnp.float32)
    weighted_sum = jnp.zeros((tok_seq, head_dim), jnp.float32)
    for block, masked, allowed in zip(got, masked_list, allowed_list):
        weights = jnp.where(allowed, jnp.exp(masked - run_max[:, None]), 0.0)
        run_total = run_total + jnp.sum(weights, axis=1)
        weighted_sum = weighted_sum + jnp.dot(
            weights.astype(jnp.bfloat16), block[:tok_seq, head_dim:], preferred_element_type=jnp.float32
        )
    head_out = (weighted_sum / run_total[:, None]).astype(jnp.bfloat16)
    partial_value = jnp.dot(head_out, w_out, preferred_element_type=jnp.float32)
    tok_dev = tok_seq // lax.axis_size("exp")
    own_start = lax.axis_index("exp") * tok_dev
    n_exp = lax.axis_size("exp")
    exp_index = lax.axis_index("exp")
    section_sum = partial_value + lax.ppermute(
        partial_value.astype(jnp.bfloat16), "section", swap
    ).astype(jnp.float32)
    summed = jnp.where(
        section_index == 0,
        lax.dynamic_slice_in_dim(section_sum, own_start, tok_dev, 0),
        jnp.zeros((tok_dev, width), jnp.float32),
    )
    for step in range(n_exp // 2):
        pairs = []
        for core in range(2):
            shift = 2 * step + 1 + core
            if shift < n_exp:
                pairs += [(core * n_exp + j, core * n_exp + (j + shift) % n_exp) for j in range(n_exp)]
        target = (exp_index + 2 * step + 1 + section_index) % n_exp
        chunk = lax.dynamic_slice_in_dim(section_sum, target * tok_dev, tok_dev, 0)
        summed = summed + lax.ppermute(
            chunk.astype(jnp.bfloat16), ("section", "exp"), pairs
        ).astype(jnp.float32)
    summed = summed + lax.ppermute(summed, "section", swap)
    own_rows = lax.dynamic_slice_in_dim(hidden_in, own_start, tok_dev, 0)
    residual = (own_rows.astype(jnp.float32) + summed).astype(jnp.bfloat16)
    moe_in = rms_scale(residual, moe_gain)
    experts = lax.axis_size("seq") * lax.axis_size("exp") // 2
    top_count = expert_ids.shape[1]
    capacity = min(tok_dev, max(2, 2 * tok_dev * top_count // experts))
    row_count = tok_dev * top_count
    flat_ids = expert_ids.reshape(row_count)
    one_hot = (flat_ids[:, None] == jnp.arange(experts, dtype=jnp.int32)[None, :]).astype(jnp.int32)
    slot_rank = jnp.sum((jnp.cumsum(one_hot, axis=0) - one_hot) * one_hot, axis=1)
    slot_index = flat_ids * capacity + slot_rank
    placed = slot_index[:, None] == jnp.arange(experts * capacity, dtype=jnp.int32)[None, :]
    repeated = jnp.repeat(moe_in, top_count, axis=0)
    outgoing = lax.dot_general(
        placed.astype(jnp.bfloat16),
        repeated,
        (((0,), (0,)), ((), ())),
        preferred_element_type=jnp.float32,
    ).astype(jnp.bfloat16)
    row_token = jnp.arange(row_count, dtype=jnp.int32) // top_count
    token_hot = (row_token[None, :] == jnp.arange(tok_dev, dtype=jnp.int32)[:, None]).astype(
        jnp.float32
    )
    weighted = token_hot * route_weights.reshape(row_count)[None, :]
    combine = jnp.dot(weighted, placed.astype(jnp.float32), precision=lax.Precision.HIGHEST)
    half_cap = capacity // 2
    own_half = lax.dynamic_slice_in_dim(
        outgoing.reshape(experts, capacity, width), section_index * half_cap, half_cap, 1
    )
    doubled = jnp.broadcast_to(
        own_half.reshape(experts, 1, half_cap, width), (experts, 2, half_cap, width)
    ).reshape(2 * experts, half_cap, width)
    arrived = lax.all_to_all(doubled, ("seq", "exp"), split_axis=0, concat_axis=0, tiled=True)
    partner = lax.ppermute(arrived, "section", [(0, 1), (1, 0)])

    def quarter_ffn(rows):
        gate_proj = jnp.dot(rows, gate_halves[0], preferred_element_type=jnp.float32)
        up_proj = jnp.dot(rows, up_halves[0], preferred_element_type=jnp.float32)
        activated = (jax.nn.silu(gate_proj) * up_proj).astype(jnp.bfloat16)
        return jnp.dot(activated, down_halves[0], preferred_element_type=jnp.float32).astype(
            jnp.bfloat16
        )

    own_rows_out = quarter_ffn(arrived.reshape(-1, width))
    partner_rows_out = quarter_ffn(partner.reshape(-1, width))
    pair_sum = own_rows_out.astype(jnp.float32) + lax.ppermute(
        partner_rows_out, "section", [(0, 1), (1, 0)]
    ).astype(jnp.float32)
    returned = lax.all_to_all(
        pair_sum.astype(jnp.bfloat16).reshape(arrived.shape),
        ("seq", "exp"),
        split_axis=0,
        concat_axis=0,
        tiled=True,
    )
    halves_sum = jnp.sum(
        returned.reshape(experts, 2, half_cap, width).astype(jnp.float32), axis=1
    ).reshape(experts * half_cap, width)
    own_combine = lax.dynamic_slice_in_dim(
        combine.reshape(tok_dev, experts, capacity), section_index * half_cap, half_cap, 2
    ).reshape(tok_dev, experts * half_cap)
    moe_part = jnp.dot(own_combine, halves_sum, precision=lax.Precision.HIGHEST)
    moe_total = moe_part + lax.ppermute(moe_part, "section", [(0, 1), (1, 0)])
    return (residual.astype(jnp.float32) + moe_total).astype(jnp.bfloat16)


def solution(mesh):
    in_specs = (
        P("seq", None),
        P("seq"),
        P(),
        P(None, ("section", "exp")),
        P(None, ("section", "exp")),
        P(None, ("section", "exp")),
        P(("section", "exp"), None),
        P(),
        P(("seq", "exp"), None),
        P(("seq", "exp"), None),
        P(("seq", "exp"), None, "section"),
        P(("seq", "exp"), None, "section"),
        P(("seq", "exp"), "section", None),
    )
    out_specs = P(("seq", "exp"), None)
    return jax.shard_map(
        per_device, mesh=mesh, in_specs=in_specs, out_specs=out_specs, check_vma=False
    )
```

```python
import math

import jax
import jax.numpy as jnp
from jax import lax
from jax.sharding import PartitionSpec as P

epsilon = 1e-05
rope_base = 10000.0
prompt_max = 1024


def rms_scale(rows, gain):
    wide = rows.astype(jnp.float32)
    inverse = lax.rsqrt(jnp.mean(wide * wide, axis=-1, keepdims=True) + epsilon)
    return (wide * inverse * gain).astype(jnp.bfloat16)


def rotate(values, positions):
    half_dim = values.shape[-1] // 2
    frequency = rope_base ** (-2.0 * jnp.arange(half_dim, dtype=jnp.float32) / values.shape[-1])
    angles = positions.astype(jnp.float32)[:, None] * frequency[None, :]
    cosine = jnp.cos(angles)
    sine_part = jnp.sin(angles)
    first_half = values[:, :half_dim]
    second_half = values[:, half_dim:]
    return jnp.concatenate(
        [
            first_half * cosine - second_half * sine_part,
            second_half * cosine + first_half * sine_part,
        ],
        axis=-1,
    )


def per_device(
    hidden_in,
    seg_ids,
    attn_gain,
    w_query,
    w_key,
    w_value,
    w_out,
    moe_gain,
    expert_ids,
    route_weights,
    gate_halves,
    up_halves,
    down_halves,
):
    tok_seq = hidden_in.shape[0]
    width = hidden_in.shape[1]
    head_dim = w_query.shape[1]
    positions = lax.axis_index("seq") * tok_seq + jnp.arange(tok_seq, dtype=jnp.int32)
    normed = rms_scale(hidden_in, attn_gain)
    query_rows = rotate(
        jnp.dot(normed, w_query, preferred_element_type=jnp.float32), positions
    ).astype(jnp.bfloat16)
    key_rows = rotate(jnp.dot(normed, w_key, preferred_element_type=jnp.float32), positions).astype(
        jnp.bfloat16
    )
    value_rows = jnp.dot(normed, w_value, preferred_element_type=jnp.float32).astype(jnp.bfloat16)
    score_scale = 1.0 / math.sqrt(head_dim)
    n_seq = lax.axis_size("seq")
    seq_index = lax.axis_index("seq")
    window = min(n_seq - 1, -(-(prompt_max - 1) // tok_seq))
    seg_rows = jnp.zeros((16, 2 * head_dim), jnp.bfloat16)
    seg_rows = seg_rows.at[0, :tok_seq].set(seg_ids.astype(jnp.bfloat16))
    packed = jnp.concatenate([jnp.concatenate([key_rows, value_rows], axis=1), seg_rows], axis=0)
    section_index = lax.axis_index("section")
    swap = [(0, 1), (1, 0)]
    lag = jnp.arange(n_seq, dtype=jnp.int32) - seq_index
    outbound = jnp.where(
        ((lag >= 0) & (lag <= window))[:, None, None], packed[None], jnp.zeros_like(packed)[None]
    )
    inbound = lax.all_to_all(outbound, "seq", split_axis=0, concat_axis=0, tiled=True)
    got = [
        lax.dynamic_index_in_dim(inbound, jnp.maximum(seq_index - shift, 0), 0, keepdims=False)
        for shift in range(window + 1)
    ]
    masked_list = []
    allowed_list = []
    for shift, block in enumerate(got):
        piece_keys = block[:tok_seq, :head_dim]
        key_segs = block[tok_seq, :tok_seq].astype(jnp.int32)
        scores = (
            lax.dot_general(
                query_rows, piece_keys, (((1,), (1,)), ((), ())), preferred_element_type=jnp.float32
            )
            * score_scale
        )
        key_piece = seq_index - shift
        key_pos = key_piece * tok_seq + jnp.arange(tok_seq, dtype=jnp.int32)
        allowed = (
            (seg_ids[:, None] == key_segs[None, :])
            & (key_pos[None, :] <= positions[:, None])
            & (key_piece >= 0)
        )
        masked_list.append(jnp.where(allowed, scores, -1e30))
        allowed_list.append(allowed)
    run_max = jnp.max(jnp.stack([jnp.max(m, axis=1) for m in masked_list], axis=0), axis=0)
    run_total = jnp.zeros((tok_seq,), jnp.float32)
    weighted_sum = jnp.zeros((tok_seq, head_dim), jnp.float32)
    for block, masked, allowed in zip(got, masked_list, allowed_list):
        weights = jnp.where(allowed, jnp.exp(masked - run_max[:, None]), 0.0)
        run_total = run_total + jnp.sum(weights, axis=1)
        weighted_sum = weighted_sum + jnp.dot(
            weights.astype(jnp.bfloat16), block[:tok_seq, head_dim:], preferred_element_type=jnp.float32
        )
    head_out = (weighted_sum / run_total[:, None]).astype(jnp.bfloat16)
    partial_value = jnp.dot(head_out, w_out, preferred_element_type=jnp.float32)
    tok_dev = tok_seq // lax.axis_size("exp")
    own_start = lax.axis_index("exp") * tok_dev
    n_exp = lax.axis_size("exp")
    exp_index = lax.axis_index("exp")
    section_sum = partial_value + lax.ppermute(partial_value, "section", swap)
    summed = jnp.where(
        section_index == 0,
        lax.dynamic_slice_in_dim(section_sum, own_start, tok_dev, 0),
        jnp.zeros((tok_dev, width), jnp.float32),
    )
    for step in range(n_exp // 2):
        pairs = []
        for core in range(2):
            shift = 2 * step + 1 + core
            if shift < n_exp:
                pairs += [(core * n_exp + j, core * n_exp + (j + shift) % n_exp) for j in range(n_exp)]
        target = (exp_index + 2 * step + 1 + section_index) % n_exp
        chunk = lax.dynamic_slice_in_dim(section_sum, target * tok_dev, tok_dev, 0)
        summed = summed + lax.ppermute(
            chunk.astype(jnp.bfloat16), ("section", "exp"), pairs
        ).astype(jnp.float32)
    summed = summed + lax.ppermute(summed, "section", swap)
    own_rows = lax.dynamic_slice_in_dim(hidden_in, own_start, tok_dev, 0)
    residual = (own_rows.astype(jnp.float32) + summed).astype(jnp.bfloat16)
    moe_in = rms_scale(residual, moe_gain)
    experts = lax.axis_size("seq") * lax.axis_size("exp") // 2
    top_count = expert_ids.shape[1]
    capacity = min(tok_dev, max(2, 2 * tok_dev * top_count // experts))
    row_count = tok_dev * top_count
    flat_ids = expert_ids.reshape(row_count)
    one_hot = (flat_ids[:, None] == jnp.arange(experts, dtype=jnp.int32)[None, :]).astype(jnp.int32)
    slot_rank = jnp.sum((jnp.cumsum(one_hot, axis=0) - one_hot) * one_hot, axis=1)
    slot_index = flat_ids * capacity + slot_rank
    placed = slot_index[:, None] == jnp.arange(experts * capacity, dtype=jnp.int32)[None, :]
    repeated = jnp.repeat(moe_in, top_count, axis=0)
    outgoing = lax.dot_general(
        placed.astype(jnp.bfloat16),
        repeated,
        (((0,), (0,)), ((), ())),
        preferred_element_type=jnp.float32,
    ).astype(jnp.bfloat16)
    row_token = jnp.arange(row_count, dtype=jnp.int32) // top_count
    token_hot = (row_token[None, :] == jnp.arange(tok_dev, dtype=jnp.int32)[:, None]).astype(
        jnp.float32
    )
    weighted = token_hot * route_weights.reshape(row_count)[None, :]
    combine = jnp.dot(weighted, placed.astype(jnp.float32), precision=lax.Precision.HIGHEST)
    half_cap = capacity // 2
    own_half = lax.dynamic_slice_in_dim(
        outgoing.reshape(experts, capacity, width), section_index * half_cap, half_cap, 1
    )
    doubled = jnp.broadcast_to(
        own_half.reshape(experts, 1, half_cap, width), (experts, 2, half_cap, width)
    ).reshape(2 * experts, half_cap, width)
    arrived = lax.all_to_all(doubled, ("seq", "exp"), split_axis=0, concat_axis=0, tiled=True)
    partner = lax.ppermute(arrived, "section", [(0, 1), (1, 0)])

    def quarter_ffn(rows):
        gate_proj = jnp.dot(rows, gate_halves[0], preferred_element_type=jnp.float32)
        up_proj = jnp.dot(rows, up_halves[0], preferred_element_type=jnp.float32)
        activated = (jax.nn.silu(gate_proj) * up_proj).astype(jnp.bfloat16)
        return jnp.dot(activated, down_halves[0], preferred_element_type=jnp.float32).astype(
            jnp.bfloat16
        )

    own_rows_out = quarter_ffn(arrived.reshape(-1, width))
    partner_rows_out = quarter_ffn(partner.reshape(-1, width))
    pair_sum = own_rows_out.astype(jnp.float32) + lax.ppermute(
        partner_rows_out, "section", [(0, 1), (1, 0)]
    ).astype(jnp.float32)
    returned = lax.all_to_all(
        pair_sum.astype(jnp.bfloat16).reshape(arrived.shape),
        ("seq", "exp"),
        split_axis=0,
        concat_axis=0,
        tiled=True,
    )
    halves_sum = jnp.sum(
        returned.reshape(experts, 2, half_cap, width).astype(jnp.float32), axis=1
    ).reshape(experts * half_cap, width)
    own_combine = lax.dynamic_slice_in_dim(
        combine.reshape(tok_dev, experts, capacity), section_index * half_cap, half_cap, 2
    ).reshape(tok_dev, experts * half_cap)
    moe_part = jnp.dot(own_combine, halves_sum, precision=lax.Precision.HIGHEST)
    moe_total = moe_part + lax.ppermute(moe_part, "section", [(0, 1), (1, 0)])
    return (residual.astype(jnp.float32) + moe_total).astype(jnp.bfloat16)


def solution(mesh):
    in_specs = (
        P("seq", None),
        P("seq"),
        P(),
        P(None, ("section", "exp")),
        P(None, ("section", "exp")),
        P(None, ("section", "exp")),
        P(("section", "exp"), None),
        P(),
        P(("seq", "exp"), None),
        P(("seq", "exp"), None),
        P(("seq", "exp"), None, "section"),
        P(("seq", "exp"), None, "section"),
        P(("seq", "exp"), "section", None),
    )
    out_specs = P(("seq", "exp"), None)
    return jax.shard_map(
        per_device, mesh=mesh, in_specs=in_specs, out_specs=out_specs, check_vma=False
    )
```

```python
import math

import jax
import jax.numpy as jnp
from jax import lax
from jax.sharding import PartitionSpec as P

epsilon = 1e-05
rope_base = 10000.0
prompt_max = 1024


def rms_scale(rows, gain):
    wide = rows.astype(jnp.float32)
    inverse = lax.rsqrt(jnp.mean(wide * wide, axis=-1, keepdims=True) + epsilon)
    return (wide * inverse * gain).astype(jnp.bfloat16)


def rotate(values, positions):
    half_dim = values.shape[-1] // 2
    frequency = rope_base ** (-2.0 * jnp.arange(half_dim, dtype=jnp.float32) / values.shape[-1])
    angles = positions.astype(jnp.float32)[:, None] * frequency[None, :]
    cosine = jnp.cos(angles)
    sine_part = jnp.sin(angles)
    first_half = values[:, :half_dim]
    second_half = values[:, half_dim:]
    return jnp.concatenate(
        [
            first_half * cosine - second_half * sine_part,
            second_half * cosine + first_half * sine_part,
        ],
        axis=-1,
    )


def per_device(
    hidden_in,
    seg_ids,
    attn_gain,
    w_query,
    w_key,
    w_value,
    w_out,
    moe_gain,
    expert_ids,
    route_weights,
    gate_halves,
    up_halves,
    down_halves,
):
    tok_seq = hidden_in.shape[0]
    width = hidden_in.shape[1]
    head_dim = w_query.shape[1]
    positions = lax.axis_index("seq") * tok_seq + jnp.arange(tok_seq, dtype=jnp.int32)
    normed = rms_scale(hidden_in, attn_gain)
    query_rows = rotate(
        jnp.dot(normed, w_query, preferred_element_type=jnp.float32), positions
    ).astype(jnp.bfloat16)
    key_rows = rotate(jnp.dot(normed, w_key, preferred_element_type=jnp.float32), positions).astype(
        jnp.bfloat16
    )
    value_rows = jnp.dot(normed, w_value, preferred_element_type=jnp.float32).astype(jnp.bfloat16)
    score_scale = 1.0 / math.sqrt(head_dim)
    n_seq = lax.axis_size("seq")
    seq_index = lax.axis_index("seq")
    window = min(n_seq - 1, -(-(prompt_max - 1) // tok_seq))
    seg_rows = jnp.zeros((16, 2 * head_dim), jnp.bfloat16)
    seg_rows = seg_rows.at[0, :tok_seq].set(seg_ids.astype(jnp.bfloat16))
    packed = jnp.concatenate([jnp.concatenate([key_rows, value_rows], axis=1), seg_rows], axis=0)
    section_index = lax.axis_index("section")
    swap = [(0, 1), (1, 0)]
    lag = jnp.arange(n_seq, dtype=jnp.int32) - seq_index
    outbound = jnp.where(
        ((lag >= 0) & (lag <= window))[:, None, None], packed[None], jnp.zeros_like(packed)[None]
    )
    inbound = lax.all_to_all(outbound, "seq", split_axis=0, concat_axis=0, tiled=True)
    got = [
        lax.dynamic_index_in_dim(inbound, jnp.maximum(seq_index - shift, 0), 0, keepdims=False)
        for shift in range(window + 1)
    ]
    masked_list = []
    allowed_list = []
    for shift, block in enumerate(got):
        piece_keys = block[:tok_seq, :head_dim]
        key_segs = block[tok_seq, :tok_seq].astype(jnp.int32)
        scores = (
            lax.dot_general(
                query_rows, piece_keys, (((1,), (1,)), ((), ())), preferred_element_type=jnp.float32
            )
            * score_scale
        )
        key_piece = seq_index - shift
        key_pos = key_piece * tok_seq + jnp.arange(tok_seq, dtype=jnp.int32)
        allowed = (
            (seg_ids[:, None] == key_segs[None, :])
            & (key_pos[None, :] <= positions[:, None])
            & (key_piece >= 0)
        )
        masked_list.append(jnp.where(allowed, scores, -1e30))
        allowed_list.append(allowed)
    run_max = jnp.max(jnp.stack([jnp.max(m, axis=1) for m in masked_list], axis=0), axis=0)
    run_total = jnp.zeros((tok_seq,), jnp.float32)
    weighted_sum = jnp.zeros((tok_seq, head_dim), jnp.float32)
    for block, masked, allowed in zip(got, masked_list, allowed_list):
        weights = jnp.where(allowed, jnp.exp(masked - run_max[:, None]), 0.0)
        run_total = run_total + jnp.sum(weights, axis=1)
        weighted_sum = weighted_sum + jnp.dot(
            weights.astype(jnp.bfloat16), block[:tok_seq, head_dim:], preferred_element_type=jnp.float32
        )
    head_out = (weighted_sum / run_total[:, None]).astype(jnp.bfloat16)
    partial_value = jnp.dot(head_out, w_out, preferred_element_type=jnp.float32)
    tok_dev = tok_seq // lax.axis_size("exp")
    own_start = lax.axis_index("exp") * tok_dev
    n_exp = lax.axis_size("exp")
    exp_index = lax.axis_index("exp")
    section_sum = partial_value + lax.ppermute(partial_value, "section", swap)
    half_width = width // 2
    own_cols = lax.dynamic_slice_in_dim(section_sum, section_index * half_width, half_width, 1)
    spread = lax.all_to_all(
        own_cols.astype(jnp.bfloat16).reshape(n_exp, tok_dev, half_width),
        "exp",
        split_axis=0,
        concat_axis=0,
        tiled=True,
    )
    col_sum = jnp.sum(spread.astype(jnp.float32), axis=0)
    other_cols = lax.ppermute(col_sum, "section", swap)
    summed = jnp.where(
        section_index == 0,
        jnp.concatenate([col_sum, other_cols], axis=1),
        jnp.concatenate([other_cols, col_sum], axis=1),
    )
    own_rows = lax.dynamic_slice_in_dim(hidden_in, own_start, tok_dev, 0)
    residual = (own_rows.astype(jnp.float32) + summed).astype(jnp.bfloat16)
    moe_in = rms_scale(residual, moe_gain)
    experts = lax.axis_size("seq") * lax.axis_size("exp") // 2
    top_count = expert_ids.shape[1]
    capacity = min(tok_dev, max(2, 2 * tok_dev * top_count // experts))
    row_count = tok_dev * top_count
    flat_ids = expert_ids.reshape(row_count)
    one_hot = (flat_ids[:, None] == jnp.arange(experts, dtype=jnp.int32)[None, :]).astype(jnp.int32)
    slot_rank = jnp.sum((jnp.cumsum(one_hot, axis=0) - one_hot) * one_hot, axis=1)
    slot_index = flat_ids * capacity + slot_rank
    placed = slot_index[:, None] == jnp.arange(experts * capacity, dtype=jnp.int32)[None, :]
    repeated = jnp.repeat(moe_in, top_count, axis=0)
    outgoing = lax.dot_general(
        placed.astype(jnp.bfloat16),
        repeated,
        (((0,), (0,)), ((), ())),
        preferred_element_type=jnp.float32,
    ).astype(jnp.bfloat16)
    row_token = jnp.arange(row_count, dtype=jnp.int32) // top_count
    token_hot = (row_token[None, :] == jnp.arange(tok_dev, dtype=jnp.int32)[:, None]).astype(
        jnp.float32
    )
    weighted = token_hot * route_weights.reshape(row_count)[None, :]
    combine = jnp.dot(weighted, placed.astype(jnp.float32), precision=lax.Precision.HIGHEST)
    half_cap = capacity // 2
    own_half = lax.dynamic_slice_in_dim(
        outgoing.reshape(experts, capacity, width), section_index * half_cap, half_cap, 1
    )
    doubled = jnp.broadcast_to(
        own_half.reshape(experts, 1, half_cap, width), (experts, 2, half_cap, width)
    ).reshape(2 * experts, half_cap, width)
    arrived = lax.all_to_all(doubled, ("seq", "exp"), split_axis=0, concat_axis=0, tiled=True)
    partner = lax.ppermute(arrived, "section", [(0, 1), (1, 0)])

    def quarter_ffn(rows):
        gate_proj = jnp.dot(rows, gate_halves[0], preferred_element_type=jnp.float32)
        up_proj = jnp.dot(rows, up_halves[0], preferred_element_type=jnp.float32)
        activated = (jax.nn.silu(gate_proj) * up_proj).astype(jnp.bfloat16)
        return jnp.dot(activated, down_halves[0], preferred_element_type=jnp.float32).astype(
            jnp.bfloat16
        )

    own_rows_out = quarter_ffn(arrived.reshape(-1, width))
    partner_rows_out = quarter_ffn(partner.reshape(-1, width))
    pair_sum = own_rows_out.astype(jnp.float32) + lax.ppermute(
        partner_rows_out, "section", [(0, 1), (1, 0)]
    ).astype(jnp.float32)
    returned = lax.all_to_all(
        pair_sum.astype(jnp.bfloat16).reshape(arrived.shape),
        ("seq", "exp"),
        split_axis=0,
        concat_axis=0,
        tiled=True,
    )
    halves_sum = jnp.sum(
        returned.reshape(experts, 2, half_cap, width).astype(jnp.float32), axis=1
    ).reshape(experts * half_cap, width)
    own_combine = lax.dynamic_slice_in_dim(
        combine.reshape(tok_dev, experts, capacity), section_index * half_cap, half_cap, 2
    ).reshape(tok_dev, experts * half_cap)
    moe_part = jnp.dot(own_combine, halves_sum, precision=lax.Precision.HIGHEST)
    moe_total = moe_part + lax.ppermute(moe_part, "section", [(0, 1), (1, 0)])
    return (residual.astype(jnp.float32) + moe_total).astype(jnp.bfloat16)


def solution(mesh):
    in_specs = (
        P("seq", None),
        P("seq"),
        P(),
        P(None, ("section", "exp")),
        P(None, ("section", "exp")),
        P(None, ("section", "exp")),
        P(("section", "exp"), None),
        P(),
        P(("seq", "exp"), None),
        P(("seq", "exp"), None),
        P(("seq", "exp"), None, "section"),
        P(("seq", "exp"), None, "section"),
        P(("seq", "exp"), "section", None),
    )
    out_specs = P(("seq", "exp"), None)
    return jax.shard_map(
        per_device, mesh=mesh, in_specs=in_specs, out_specs=out_specs, check_vma=False
    )
```

```python
import math

import jax
import jax.numpy as jnp
from jax import lax
from jax.sharding import PartitionSpec as P

epsilon = 1e-05
rope_base = 10000.0
prompt_max = 1024


def rms_scale(rows, gain):
    wide = rows.astype(jnp.float32)
    inverse = lax.rsqrt(jnp.mean(wide * wide, axis=-1, keepdims=True) + epsilon)
    return (wide * inverse * gain).astype(jnp.bfloat16)


def rotate(values, positions):
    half_dim = values.shape[-1] // 2
    frequency = rope_base ** (-2.0 * jnp.arange(half_dim, dtype=jnp.float32) / values.shape[-1])
    angles = positions.astype(jnp.float32)[:, None] * frequency[None, :]
    cosine = jnp.cos(angles)
    sine_part = jnp.sin(angles)
    first_half = values[:, :half_dim]
    second_half = values[:, half_dim:]
    return jnp.concatenate(
        [
            first_half * cosine - second_half * sine_part,
            second_half * cosine + first_half * sine_part,
        ],
        axis=-1,
    )


def per_device(
    hidden_in,
    seg_ids,
    attn_gain,
    w_query,
    w_key,
    w_value,
    w_out,
    moe_gain,
    expert_ids,
    route_weights,
    gate_halves,
    up_halves,
    down_halves,
):
    tok_seq = hidden_in.shape[0]
    width = hidden_in.shape[1]
    head_dim = w_query.shape[1]
    positions = lax.axis_index("seq") * tok_seq + jnp.arange(tok_seq, dtype=jnp.int32)
    normed = rms_scale(hidden_in, attn_gain)
    query_rows = rotate(
        jnp.dot(normed, w_query, preferred_element_type=jnp.float32), positions
    ).astype(jnp.bfloat16)
    key_rows = rotate(jnp.dot(normed, w_key, preferred_element_type=jnp.float32), positions).astype(
        jnp.bfloat16
    )
    value_rows = jnp.dot(normed, w_value, preferred_element_type=jnp.float32).astype(jnp.bfloat16)
    score_scale = 1.0 / math.sqrt(head_dim)
    n_seq = lax.axis_size("seq")
    seq_index = lax.axis_index("seq")
    window = min(n_seq - 1, -(-(prompt_max - 1) // tok_seq))
    seg_rows = jnp.zeros((16, 2 * head_dim), jnp.bfloat16)
    seg_rows = seg_rows.at[0, :tok_seq].set(seg_ids.astype(jnp.bfloat16))
    packed = jnp.concatenate([jnp.concatenate([key_rows, value_rows], axis=1), seg_rows], axis=0)
    section_index = lax.axis_index("section")
    swap = [(0, 1), (1, 0)]
    lag = jnp.arange(n_seq, dtype=jnp.int32) - seq_index
    outbound = jnp.where(
        ((lag >= 0) & (lag <= window))[:, None, None], packed[None], jnp.zeros_like(packed)[None]
    )
    inbound = lax.all_to_all(outbound, "seq", split_axis=0, concat_axis=0, tiled=True)
    got = [packed] + [
        lax.dynamic_index_in_dim(inbound, jnp.maximum(seq_index - shift, 0), 0, keepdims=False)
        for shift in range(1, window + 1)
    ]
    masked_list = []
    allowed_list = []
    for shift, block in enumerate(got):
        piece_keys = block[:tok_seq, :head_dim]
        key_segs = block[tok_seq, :tok_seq].astype(jnp.int32)
        scores = (
            lax.dot_general(
                query_rows, piece_keys, (((1,), (1,)), ((), ())), preferred_element_type=jnp.float32
            )
            * score_scale
        )
        key_piece = seq_index - shift
        key_pos = key_piece * tok_seq + jnp.arange(tok_seq, dtype=jnp.int32)
        allowed = (
            (seg_ids[:, None] == key_segs[None, :])
            & (key_pos[None, :] <= positions[:, None])
            & (key_piece >= 0)
        )
        masked_list.append(jnp.where(allowed, scores, -1e30))
        allowed_list.append(allowed)
    run_max = jnp.max(jnp.stack([jnp.max(m, axis=1) for m in masked_list], axis=0), axis=0)
    run_total = jnp.zeros((tok_seq,), jnp.float32)
    weighted_sum = jnp.zeros((tok_seq, head_dim), jnp.float32)
    for block, masked, allowed in zip(got, masked_list, allowed_list):
        weights = jnp.where(allowed, jnp.exp(masked - run_max[:, None]), 0.0)
        run_total = run_total + jnp.sum(weights, axis=1)
        weighted_sum = weighted_sum + jnp.dot(
            weights.astype(jnp.bfloat16), block[:tok_seq, head_dim:], preferred_element_type=jnp.float32
        )
    head_out = (weighted_sum / run_total[:, None]).astype(jnp.bfloat16)
    partial_value = jnp.dot(head_out, w_out, preferred_element_type=jnp.float32)
    tok_dev = tok_seq // lax.axis_size("exp")
    own_start = lax.axis_index("exp") * tok_dev
    n_exp = lax.axis_size("exp")
    exp_index = lax.axis_index("exp")
    section_sum = partial_value + lax.ppermute(partial_value, "section", swap)
    summed = jnp.where(
        section_index == 0,
        lax.dynamic_slice_in_dim(section_sum, own_start, tok_dev, 0),
        jnp.zeros((tok_dev, width), jnp.float32),
    )
    for step in range(n_exp // 2):
        pairs = []
        for core in range(2):
            shift = 2 * step + 1 + core
            if shift < n_exp:
                pairs += [(core * n_exp + j, core * n_exp + (j + shift) % n_exp) for j in range(n_exp)]
        target = (exp_index + 2 * step + 1 + section_index) % n_exp
        chunk = lax.dynamic_slice_in_dim(section_sum, target * tok_dev, tok_dev, 0)
        summed = summed + lax.ppermute(
            chunk.astype(jnp.bfloat16), ("section", "exp"), pairs
        ).astype(jnp.float32)
    summed = summed + lax.ppermute(summed, "section", swap)
    own_rows = lax.dynamic_slice_in_dim(hidden_in, own_start, tok_dev, 0)
    residual = (own_rows.astype(jnp.float32) + summed).astype(jnp.bfloat16)
    moe_in = rms_scale(residual, moe_gain)
    experts = lax.axis_size("seq") * lax.axis_size("exp") // 2
    top_count = expert_ids.shape[1]
    capacity = min(tok_dev, max(2, 2 * tok_dev * top_count // experts))
    row_count = tok_dev * top_count
    flat_ids = expert_ids.reshape(row_count)
    one_hot = (flat_ids[:, None] == jnp.arange(experts, dtype=jnp.int32)[None, :]).astype(jnp.int32)
    slot_rank = jnp.sum((jnp.cumsum(one_hot, axis=0) - one_hot) * one_hot, axis=1)
    slot_index = flat_ids * capacity + slot_rank
    placed = slot_index[:, None] == jnp.arange(experts * capacity, dtype=jnp.int32)[None, :]
    repeated = jnp.repeat(moe_in, top_count, axis=0)
    outgoing = lax.dot_general(
        placed.astype(jnp.bfloat16),
        repeated,
        (((0,), (0,)), ((), ())),
        preferred_element_type=jnp.float32,
    ).astype(jnp.bfloat16)
    row_token = jnp.arange(row_count, dtype=jnp.int32) // top_count
    token_hot = (row_token[None, :] == jnp.arange(tok_dev, dtype=jnp.int32)[:, None]).astype(
        jnp.float32
    )
    weighted = token_hot * route_weights.reshape(row_count)[None, :]
    combine = jnp.dot(weighted, placed.astype(jnp.float32), precision=lax.Precision.HIGHEST)
    half_cap = capacity // 2
    own_half = lax.dynamic_slice_in_dim(
        outgoing.reshape(experts, capacity, width), section_index * half_cap, half_cap, 1
    )
    doubled = jnp.broadcast_to(
        own_half.reshape(experts, 1, half_cap, width), (experts, 2, half_cap, width)
    ).reshape(2 * experts, half_cap, width)
    arrived = lax.all_to_all(doubled, ("seq", "exp"), split_axis=0, concat_axis=0, tiled=True)
    partner = lax.ppermute(arrived, "section", [(0, 1), (1, 0)])

    def quarter_ffn(rows):
        gate_proj = jnp.dot(rows, gate_halves[0], preferred_element_type=jnp.float32)
        up_proj = jnp.dot(rows, up_halves[0], preferred_element_type=jnp.float32)
        activated = (jax.nn.silu(gate_proj) * up_proj).astype(jnp.bfloat16)
        return jnp.dot(activated, down_halves[0], preferred_element_type=jnp.float32).astype(
            jnp.bfloat16
        )

    own_rows_out = quarter_ffn(arrived.reshape(-1, width))
    partner_rows_out = quarter_ffn(partner.reshape(-1, width))
    pair_sum = own_rows_out.astype(jnp.float32) + lax.ppermute(
        partner_rows_out, "section", [(0, 1), (1, 0)]
    ).astype(jnp.float32)
    returned = lax.all_to_all(
        pair_sum.astype(jnp.bfloat16).reshape(arrived.shape),
        ("seq", "exp"),
        split_axis=0,
        concat_axis=0,
        tiled=True,
    )
    halves_sum = jnp.sum(
        returned.reshape(experts, 2, half_cap, width).astype(jnp.float32), axis=1
    ).reshape(experts * half_cap, width)
    own_combine = lax.dynamic_slice_in_dim(
        combine.reshape(tok_dev, experts, capacity), section_index * half_cap, half_cap, 2
    ).reshape(tok_dev, experts * half_cap)
    moe_part = jnp.dot(own_combine, halves_sum, precision=lax.Precision.HIGHEST)
    moe_total = moe_part + lax.ppermute(moe_part, "section", [(0, 1), (1, 0)])
    return (residual.astype(jnp.float32) + moe_total).astype(jnp.bfloat16)


def solution(mesh):
    in_specs = (
        P("seq", None),
        P("seq"),
        P(),
        P(None, ("section", "exp")),
        P(None, ("section", "exp")),
        P(None, ("section", "exp")),
        P(("section", "exp"), None),
        P(),
        P(("seq", "exp"), None),
        P(("seq", "exp"), None),
        P(("seq", "exp"), None, "section"),
        P(("seq", "exp"), None, "section"),
        P(("seq", "exp"), "section", None),
    )
    out_specs = P(("seq", "exp"), None)
    return jax.shard_map(
        per_device, mesh=mesh, in_specs=in_specs, out_specs=out_specs, check_vma=False
    )
```

```python
import math

import jax
import jax.numpy as jnp
from jax import lax
from jax.sharding import PartitionSpec as P

epsilon = 1e-05
rope_base = 10000.0
prompt_max = 1024


def rms_scale(rows, gain):
    wide = rows.astype(jnp.float32)
    inverse = lax.rsqrt(jnp.mean(wide * wide, axis=-1, keepdims=True) + epsilon)
    return (wide * inverse * gain).astype(jnp.bfloat16)


def rotate(values, positions):
    half_dim = values.shape[-1] // 2
    frequency = rope_base ** (-2.0 * jnp.arange(half_dim, dtype=jnp.float32) / values.shape[-1])
    angles = positions.astype(jnp.float32)[:, None] * frequency[None, :]
    cosine = jnp.cos(angles)
    sine_part = jnp.sin(angles)
    first_half = values[:, :half_dim]
    second_half = values[:, half_dim:]
    return jnp.concatenate(
        [
            first_half * cosine - second_half * sine_part,
            second_half * cosine + first_half * sine_part,
        ],
        axis=-1,
    )


def per_device(
    hidden_in,
    seg_ids,
    attn_gain,
    w_query,
    w_key,
    w_value,
    w_out,
    moe_gain,
    expert_ids,
    route_weights,
    gate_halves,
    up_halves,
    down_halves,
):
    tok_seq = hidden_in.shape[0]
    width = hidden_in.shape[1]
    head_dim = w_query.shape[1]
    positions = lax.axis_index("seq") * tok_seq + jnp.arange(tok_seq, dtype=jnp.int32)
    normed = rms_scale(hidden_in, attn_gain)
    query_rows = rotate(
        jnp.dot(normed, w_query, preferred_element_type=jnp.float32), positions
    ).astype(jnp.bfloat16)
    key_rows = rotate(jnp.dot(normed, w_key, preferred_element_type=jnp.float32), positions).astype(
        jnp.bfloat16
    )
    value_rows = jnp.dot(normed, w_value, preferred_element_type=jnp.float32).astype(jnp.bfloat16)
    score_scale = 1.0 / math.sqrt(head_dim)
    n_seq = lax.axis_size("seq")
    seq_index = lax.axis_index("seq")
    window = min(n_seq - 1, -(-(prompt_max - 1) // tok_seq))
    seg_rows = jnp.zeros((16, 2 * head_dim), jnp.bfloat16)
    seg_rows = seg_rows.at[0, :tok_seq].set(seg_ids.astype(jnp.bfloat16))
    packed = jnp.concatenate([jnp.concatenate([key_rows, value_rows], axis=1), seg_rows], axis=0)
    section_index = lax.axis_index("section")
    swap = [(0, 1), (1, 0)]
    lag = jnp.arange(n_seq, dtype=jnp.int32) - seq_index
    outbound = jnp.where(
        ((lag >= 0) & (lag <= window))[:, None, None], packed[None], jnp.zeros_like(packed)[None]
    )
    inbound = lax.all_to_all(outbound, "seq", split_axis=0, concat_axis=0, tiled=True)
    got = [packed] + [
        lax.dynamic_index_in_dim(inbound, jnp.maximum(seq_index - shift, 0), 0, keepdims=False)
        for shift in range(1, window + 1)
    ]
    masked_list = []
    allowed_list = []
    for shift, block in enumerate(got):
        piece_keys = block[:tok_seq, :head_dim]
        key_segs = block[tok_seq, :tok_seq].astype(jnp.int32)
        scores = (
            lax.dot_general(
                query_rows, piece_keys, (((1,), (1,)), ((), ())), preferred_element_type=jnp.float32
            )
            * score_scale
        )
        key_piece = seq_index - shift
        key_pos = key_piece * tok_seq + jnp.arange(tok_seq, dtype=jnp.int32)
        allowed = (
            (seg_ids[:, None] == key_segs[None, :])
            & (key_pos[None, :] <= positions[:, None])
            & (key_piece >= 0)
        )
        masked_list.append(jnp.where(allowed, scores, -1e30))
        allowed_list.append(allowed)
    run_max = jnp.max(jnp.stack([jnp.max(m, axis=1) for m in masked_list], axis=0), axis=0)
    run_total = jnp.zeros((tok_seq,), jnp.float32)
    weighted_sum = jnp.zeros((tok_seq, head_dim), jnp.float32)
    for block, masked, allowed in zip(got, masked_list, allowed_list):
        weights = jnp.where(allowed, jnp.exp(masked - run_max[:, None]), 0.0)
        run_total = run_total + jnp.sum(weights, axis=1)
        weighted_sum = weighted_sum + jnp.dot(
            weights.astype(jnp.bfloat16), block[:tok_seq, head_dim:], preferred_element_type=jnp.float32
        )
    head_out = (weighted_sum / run_total[:, None]).astype(jnp.bfloat16)
    partial_value = jnp.dot(head_out, w_out, preferred_element_type=jnp.float32)
    tok_dev = tok_seq // lax.axis_size("exp")
    own_start = lax.axis_index("exp") * tok_dev
    n_exp = lax.axis_size("exp")
    exp_index = lax.axis_index("exp")
    section_sum = partial_value + lax.ppermute(partial_value, "section", swap)
    summed = jnp.where(
        section_index == 0,
        lax.dynamic_slice_in_dim(section_sum, own_start, tok_dev, 0),
        jnp.zeros((tok_dev, width), jnp.float32),
    )
    for step in range(n_exp // 2):
        pairs = []
        for core in range(2):
            shift = 2 * step + 1 + core
            if shift < n_exp:
                pairs += [(core * n_exp + j, core * n_exp + (j + shift) % n_exp) for j in range(n_exp)]
        target = (exp_index + 2 * step + 1 + section_index) % n_exp
        chunk = lax.dynamic_slice_in_dim(section_sum, target * tok_dev, tok_dev, 0)
        summed = summed + lax.ppermute(
            chunk.astype(jnp.bfloat16), ("section", "exp"), pairs
        ).astype(jnp.float32)
    summed = summed + lax.ppermute(summed, "section", swap)
    own_rows = lax.dynamic_slice_in_dim(hidden_in, own_start, tok_dev, 0)
    residual = (own_rows.astype(jnp.float32) + summed).astype(jnp.bfloat16)
    moe_in = rms_scale(residual, moe_gain)
    experts = lax.axis_size("seq") * lax.axis_size("exp") // 2
    top_count = expert_ids.shape[1]
    capacity = min(tok_dev, max(2, 2 * tok_dev * top_count // experts))
    row_count = tok_dev * top_count
    flat_ids = expert_ids.reshape(row_count)
    one_hot = (flat_ids[:, None] == jnp.arange(experts, dtype=jnp.int32)[None, :]).astype(jnp.int32)
    slot_rank = jnp.sum((jnp.cumsum(one_hot, axis=0) - one_hot) * one_hot, axis=1)
    slot_index = flat_ids * capacity + slot_rank
    placed = slot_index[:, None] == jnp.arange(experts * capacity, dtype=jnp.int32)[None, :]
    repeated = jnp.repeat(moe_in, top_count, axis=0)
    outgoing = lax.dot_general(
        placed.astype(jnp.bfloat16),
        repeated,
        (((0,), (0,)), ((), ())),
        preferred_element_type=jnp.float32,
    ).astype(jnp.bfloat16)
    row_token = jnp.arange(row_count, dtype=jnp.int32) // top_count
    token_hot = (row_token[None, :] == jnp.arange(tok_dev, dtype=jnp.int32)[:, None]).astype(
        jnp.float32
    )
    weighted = token_hot * route_weights.reshape(row_count)[None, :]
    combine = jnp.dot(weighted, placed.astype(jnp.float32), precision=lax.Precision.HIGHEST)
    half_cap = capacity // 2
    own_half = lax.dynamic_slice_in_dim(
        outgoing.reshape(experts, capacity, width), section_index * half_cap, half_cap, 1
    )
    doubled = jnp.broadcast_to(
        own_half.reshape(experts, 1, half_cap, width), (experts, 2, half_cap, width)
    ).reshape(2 * experts, half_cap, width)
    arrived = lax.all_to_all(doubled, ("seq", "exp"), split_axis=0, concat_axis=0, tiled=True)
    partner = lax.ppermute(arrived, "section", [(0, 1), (1, 0)])

    def quarter_ffn(rows):
        gate_proj = jnp.dot(rows, gate_halves[0], preferred_element_type=jnp.float32)
        up_proj = jnp.dot(rows, up_halves[0], preferred_element_type=jnp.float32)
        activated = (jax.nn.silu(gate_proj) * up_proj).astype(jnp.bfloat16)
        return jnp.dot(activated, down_halves[0], preferred_element_type=jnp.float32).astype(
            jnp.bfloat16
        )

    own_rows_out = quarter_ffn(arrived.reshape(-1, width))
    own_rows_out, partner = lax.optimization_barrier((own_rows_out, partner))
    partner_rows_out = quarter_ffn(partner.reshape(-1, width))
    pair_sum = own_rows_out.astype(jnp.float32) + lax.ppermute(
        partner_rows_out, "section", [(0, 1), (1, 0)]
    ).astype(jnp.float32)
    returned = lax.all_to_all(
        pair_sum.astype(jnp.bfloat16).reshape(arrived.shape),
        ("seq", "exp"),
        split_axis=0,
        concat_axis=0,
        tiled=True,
    )
    halves_sum = jnp.sum(
        returned.reshape(experts, 2, half_cap, width).astype(jnp.float32), axis=1
    ).reshape(experts * half_cap, width)
    own_combine = lax.dynamic_slice_in_dim(
        combine.reshape(tok_dev, experts, capacity), section_index * half_cap, half_cap, 2
    ).reshape(tok_dev, experts * half_cap)
    moe_part = jnp.dot(own_combine, halves_sum, precision=lax.Precision.HIGHEST)
    moe_total = moe_part + lax.ppermute(moe_part, "section", [(0, 1), (1, 0)])
    return (residual.astype(jnp.float32) + moe_total).astype(jnp.bfloat16)


def solution(mesh):
    in_specs = (
        P("seq", None),
        P("seq"),
        P(),
        P(None, ("section", "exp")),
        P(None, ("section", "exp")),
        P(None, ("section", "exp")),
        P(("section", "exp"), None),
        P(),
        P(("seq", "exp"), None),
        P(("seq", "exp"), None),
        P(("seq", "exp"), None, "section"),
        P(("seq", "exp"), None, "section"),
        P(("seq", "exp"), "section", None),
    )
    out_specs = P(("seq", "exp"), None)
    return jax.shard_map(
        per_device, mesh=mesh, in_specs=in_specs, out_specs=out_specs, check_vma=False
    )
```

```python
import math

import jax
import jax.numpy as jnp
from jax import lax
from jax.sharding import PartitionSpec as P

epsilon = 1e-05
rope_base = 10000.0
prompt_max = 1024


def rms_scale(rows, gain):
    wide = rows.astype(jnp.float32)
    inverse = lax.rsqrt(jnp.mean(wide * wide, axis=-1, keepdims=True) + epsilon)
    return (wide * inverse * gain).astype(jnp.bfloat16)


def rotate(values, positions):
    half_dim = values.shape[-1] // 2
    frequency = rope_base ** (-2.0 * jnp.arange(half_dim, dtype=jnp.float32) / values.shape[-1])
    angles = positions.astype(jnp.float32)[:, None] * frequency[None, :]
    cosine = jnp.cos(angles)
    sine_part = jnp.sin(angles)
    first_half = values[:, :half_dim]
    second_half = values[:, half_dim:]
    return jnp.concatenate(
        [
            first_half * cosine - second_half * sine_part,
            second_half * cosine + first_half * sine_part,
        ],
        axis=-1,
    )


def per_device(
    hidden_in,
    seg_ids,
    attn_gain,
    w_query,
    w_key,
    w_value,
    w_out,
    moe_gain,
    expert_ids,
    route_weights,
    gate_halves,
    up_halves,
    down_halves,
):
    tok_seq = hidden_in.shape[0]
    width = hidden_in.shape[1]
    head_dim = w_query.shape[1]
    positions = lax.axis_index("seq") * tok_seq + jnp.arange(tok_seq, dtype=jnp.int32)
    normed = rms_scale(hidden_in, attn_gain)
    query_rows = rotate(
        jnp.dot(normed, w_query, preferred_element_type=jnp.float32), positions
    ).astype(jnp.bfloat16)
    key_rows = rotate(jnp.dot(normed, w_key, preferred_element_type=jnp.float32), positions).astype(
        jnp.bfloat16
    )
    value_rows = jnp.dot(normed, w_value, preferred_element_type=jnp.float32).astype(jnp.bfloat16)
    score_scale = 1.0 / math.sqrt(head_dim)
    n_seq = lax.axis_size("seq")
    seq_index = lax.axis_index("seq")
    window = min(n_seq - 1, -(-(prompt_max - 1) // tok_seq))
    seg_rows = jnp.zeros((16, 2 * head_dim), jnp.bfloat16)
    seg_rows = seg_rows.at[0, :tok_seq].set(seg_ids.astype(jnp.bfloat16))
    packed = jnp.concatenate([jnp.concatenate([key_rows, value_rows], axis=1), seg_rows], axis=0)
    section_index = lax.axis_index("section")
    swap = [(0, 1), (1, 0)]
    lag = jnp.arange(n_seq, dtype=jnp.int32) - seq_index
    outbound = jnp.where(
        ((lag >= 0) & (lag <= window))[:, None, None], packed[None], jnp.zeros_like(packed)[None]
    )
    inbound = lax.all_to_all(outbound, "seq", split_axis=0, concat_axis=0, tiled=True)
    tok_dev = tok_seq // lax.axis_size("exp")
    experts = lax.axis_size("seq") * lax.axis_size("exp") // 2
    top_count = expert_ids.shape[1]
    capacity = min(tok_dev, max(2, 2 * tok_dev * top_count // experts))
    row_count = tok_dev * top_count
    flat_ids = expert_ids.reshape(row_count)
    one_hot = (flat_ids[:, None] == jnp.arange(experts, dtype=jnp.int32)[None, :]).astype(jnp.int32)
    slot_rank = jnp.sum((jnp.cumsum(one_hot, axis=0) - one_hot) * one_hot, axis=1)
    slot_index = flat_ids * capacity + slot_rank
    placed = slot_index[:, None] == jnp.arange(experts * capacity, dtype=jnp.int32)[None, :]
    row_token = jnp.arange(row_count, dtype=jnp.int32) // top_count
    token_hot = (row_token[None, :] == jnp.arange(tok_dev, dtype=jnp.int32)[:, None]).astype(
        jnp.float32
    )
    weighted = token_hot * route_weights.reshape(row_count)[None, :]
    combine = jnp.dot(weighted, placed.astype(jnp.float32), precision=lax.Precision.HIGHEST)
    inbound, placed, combine = lax.optimization_barrier((inbound, placed, combine))
    got = [packed] + [
        lax.dynamic_index_in_dim(inbound, jnp.maximum(seq_index - shift, 0), 0, keepdims=False)
        for shift in range(1, window + 1)
    ]
    masked_list = []
    allowed_list = []
    for shift, block in enumerate(got):
        piece_keys = block[:tok_seq, :head_dim]
        key_segs = block[tok_seq, :tok_seq].astype(jnp.int32)
        scores = (
            lax.dot_general(
                query_rows, piece_keys, (((1,), (1,)), ((), ())), preferred_element_type=jnp.float32
            )
            * score_scale
        )
        key_piece = seq_index - shift
        key_pos = key_piece * tok_seq + jnp.arange(tok_seq, dtype=jnp.int32)
        allowed = (
            (seg_ids[:, None] == key_segs[None, :])
            & (key_pos[None, :] <= positions[:, None])
            & (key_piece >= 0)
        )
        masked_list.append(jnp.where(allowed, scores, -1e30))
        allowed_list.append(allowed)
    run_max = jnp.max(jnp.stack([jnp.max(m, axis=1) for m in masked_list], axis=0), axis=0)
    run_total = jnp.zeros((tok_seq,), jnp.float32)
    weighted_sum = jnp.zeros((tok_seq, head_dim), jnp.float32)
    for block, masked, allowed in zip(got, masked_list, allowed_list):
        weights = jnp.where(allowed, jnp.exp(masked - run_max[:, None]), 0.0)
        run_total = run_total + jnp.sum(weights, axis=1)
        weighted_sum = weighted_sum + jnp.dot(
            weights.astype(jnp.bfloat16), block[:tok_seq, head_dim:], preferred_element_type=jnp.float32
        )
    head_out = (weighted_sum / run_total[:, None]).astype(jnp.bfloat16)
    partial_value = jnp.dot(head_out, w_out, preferred_element_type=jnp.float32)
    own_start = lax.axis_index("exp") * tok_dev
    n_exp = lax.axis_size("exp")
    exp_index = lax.axis_index("exp")
    section_sum = partial_value + lax.ppermute(partial_value, "section", swap)
    summed = jnp.where(
        section_index == 0,
        lax.dynamic_slice_in_dim(section_sum, own_start, tok_dev, 0),
        jnp.zeros((tok_dev, width), jnp.float32),
    )
    for step in range(n_exp // 2):
        pairs = []
        for core in range(2):
            shift = 2 * step + 1 + core
            if shift < n_exp:
                pairs += [(core * n_exp + j, core * n_exp + (j + shift) % n_exp) for j in range(n_exp)]
        target = (exp_index + 2 * step + 1 + section_index) % n_exp
        chunk = lax.dynamic_slice_in_dim(section_sum, target * tok_dev, tok_dev, 0)
        summed = summed + lax.ppermute(
            chunk.astype(jnp.bfloat16), ("section", "exp"), pairs
        ).astype(jnp.float32)
    summed = summed + lax.ppermute(summed, "section", swap)
    own_rows = lax.dynamic_slice_in_dim(hidden_in, own_start, tok_dev, 0)
    residual = (own_rows.astype(jnp.float32) + summed).astype(jnp.bfloat16)
    moe_in = rms_scale(residual, moe_gain)
    repeated = jnp.repeat(moe_in, top_count, axis=0)
    outgoing = lax.dot_general(
        placed.astype(jnp.bfloat16),
        repeated,
        (((0,), (0,)), ((), ())),
        preferred_element_type=jnp.float32,
    ).astype(jnp.bfloat16)
    half_cap = capacity // 2
    own_half = lax.dynamic_slice_in_dim(
        outgoing.reshape(experts, capacity, width), section_index * half_cap, half_cap, 1
    )
    doubled = jnp.broadcast_to(
        own_half.reshape(experts, 1, half_cap, width), (experts, 2, half_cap, width)
    ).reshape(2 * experts, half_cap, width)
    arrived = lax.all_to_all(doubled, ("seq", "exp"), split_axis=0, concat_axis=0, tiled=True)
    partner = lax.ppermute(arrived, "section", [(0, 1), (1, 0)])

    def quarter_ffn(rows):
        gate_proj = jnp.dot(rows, gate_halves[0], preferred_element_type=jnp.float32)
        up_proj = jnp.dot(rows, up_halves[0], preferred_element_type=jnp.float32)
        activated = (jax.nn.silu(gate_proj) * up_proj).astype(jnp.bfloat16)
        return jnp.dot(activated, down_halves[0], preferred_element_type=jnp.float32).astype(
            jnp.bfloat16
        )

    own_rows_out = quarter_ffn(arrived.reshape(-1, width))
    own_rows_out, partner = lax.optimization_barrier((own_rows_out, partner))
    partner_rows_out = quarter_ffn(partner.reshape(-1, width))
    pair_sum = own_rows_out.astype(jnp.float32) + lax.ppermute(
        partner_rows_out, "section", [(0, 1), (1, 0)]
    ).astype(jnp.float32)
    returned = lax.all_to_all(
        pair_sum.astype(jnp.bfloat16).reshape(arrived.shape),
        ("seq", "exp"),
        split_axis=0,
        concat_axis=0,
        tiled=True,
    )
    halves_sum = jnp.sum(
        returned.reshape(experts, 2, half_cap, width).astype(jnp.float32), axis=1
    ).reshape(experts * half_cap, width)
    own_combine = lax.dynamic_slice_in_dim(
        combine.reshape(tok_dev, experts, capacity), section_index * half_cap, half_cap, 2
    ).reshape(tok_dev, experts * half_cap)
    moe_part = jnp.dot(own_combine, halves_sum, precision=lax.Precision.HIGHEST)
    moe_total = moe_part + lax.ppermute(moe_part, "section", [(0, 1), (1, 0)])
    return (residual.astype(jnp.float32) + moe_total).astype(jnp.bfloat16)


def solution(mesh):
    in_specs = (
        P("seq", None),
        P("seq"),
        P(),
        P(None, ("section", "exp")),
        P(None, ("section", "exp")),
        P(None, ("section", "exp")),
        P(("section", "exp"), None),
        P(),
        P(("seq", "exp"), None),
        P(("seq", "exp"), None),
        P(("seq", "exp"), None, "section"),
        P(("seq", "exp"), None, "section"),
        P(("seq", "exp"), "section", None),
    )
    out_specs = P(("seq", "exp"), None)
    return jax.shard_map(
        per_device, mesh=mesh, in_specs=in_specs, out_specs=out_specs, check_vma=False
    )
```

```python
import math

import jax
import jax.numpy as jnp
from jax import lax
from jax.sharding import PartitionSpec as P

epsilon = 1e-05
rope_base = 10000.0
prompt_max = 1024


def rms_scale(rows, gain):
    wide = rows.astype(jnp.float32)
    inverse = lax.rsqrt(jnp.mean(wide * wide, axis=-1, keepdims=True) + epsilon)
    return (wide * inverse * gain).astype(jnp.bfloat16)


def rotate(values, positions):
    half_dim = values.shape[-1] // 2
    frequency = rope_base ** (-2.0 * jnp.arange(half_dim, dtype=jnp.float32) / values.shape[-1])
    angles = positions.astype(jnp.float32)[:, None] * frequency[None, :]
    cosine = jnp.cos(angles)
    sine_part = jnp.sin(angles)
    first_half = values[:, :half_dim]
    second_half = values[:, half_dim:]
    return jnp.concatenate(
        [
            first_half * cosine - second_half * sine_part,
            second_half * cosine + first_half * sine_part,
        ],
        axis=-1,
    )


def per_device(
    hidden_in,
    seg_ids,
    attn_gain,
    w_query,
    w_key,
    w_value,
    w_out,
    moe_gain,
    expert_ids,
    route_weights,
    gate_halves,
    up_halves,
    down_halves,
):
    tok_seq = hidden_in.shape[0]
    width = hidden_in.shape[1]
    head_dim = w_query.shape[1]
    positions = lax.axis_index("seq") * tok_seq + jnp.arange(tok_seq, dtype=jnp.int32)
    normed = rms_scale(hidden_in, attn_gain)
    query_rows = rotate(
        jnp.dot(normed, w_query, preferred_element_type=jnp.float32), positions
    ).astype(jnp.bfloat16)
    key_rows = rotate(jnp.dot(normed, w_key, preferred_element_type=jnp.float32), positions).astype(
        jnp.bfloat16
    )
    value_rows = jnp.dot(normed, w_value, preferred_element_type=jnp.float32).astype(jnp.bfloat16)
    score_scale = 1.0 / math.sqrt(head_dim)
    n_seq = lax.axis_size("seq")
    seq_index = lax.axis_index("seq")
    window = min(n_seq - 1, -(-(prompt_max - 1) // tok_seq))
    seg_rows = jnp.zeros((16, 2 * head_dim), jnp.bfloat16)
    seg_rows = seg_rows.at[0, :tok_seq].set(seg_ids.astype(jnp.bfloat16))
    packed = jnp.concatenate([jnp.concatenate([key_rows, value_rows], axis=1), seg_rows], axis=0)
    section_index = lax.axis_index("section")
    swap = [(0, 1), (1, 0)]
    lag = jnp.arange(n_seq, dtype=jnp.int32) - seq_index
    outbound = jnp.where(
        ((lag >= 0) & (lag <= window))[:, None, None], packed[None], jnp.zeros_like(packed)[None]
    )
    inbound = lax.all_to_all(outbound, "seq", split_axis=0, concat_axis=0, tiled=True)
    got = [packed] + [
        lax.dynamic_index_in_dim(inbound, jnp.maximum(seq_index - shift, 0), 0, keepdims=False)
        for shift in range(1, window + 1)
    ]
    masked_list = []
    allowed_list = []
    for shift, block in enumerate(got):
        piece_keys = block[:tok_seq, :head_dim]
        key_segs = block[tok_seq, :tok_seq].astype(jnp.int32)
        scores = (
            lax.dot_general(
                query_rows, piece_keys, (((1,), (1,)), ((), ())), preferred_element_type=jnp.float32
            )
            * score_scale
        )
        key_piece = seq_index - shift
        key_pos = key_piece * tok_seq + jnp.arange(tok_seq, dtype=jnp.int32)
        allowed = (
            (seg_ids[:, None] == key_segs[None, :])
            & (key_pos[None, :] <= positions[:, None])
            & (key_piece >= 0)
        )
        masked_list.append(jnp.where(allowed, scores, -1e30))
        allowed_list.append(allowed)
    run_max = jnp.max(jnp.stack([jnp.max(m, axis=1) for m in masked_list], axis=0), axis=0)
    run_total = jnp.zeros((tok_seq,), jnp.float32)
    weighted_sum = jnp.zeros((tok_seq, head_dim), jnp.float32)
    for block, masked, allowed in zip(got, masked_list, allowed_list):
        weights = jnp.where(allowed, jnp.exp(masked - run_max[:, None]), 0.0)
        run_total = run_total + jnp.sum(weights, axis=1)
        weighted_sum = weighted_sum + jnp.dot(
            weights.astype(jnp.bfloat16), block[:tok_seq, head_dim:], preferred_element_type=jnp.float32
        )
    head_out = (weighted_sum / run_total[:, None]).astype(jnp.bfloat16)
    partial_value = jnp.dot(head_out, w_out, preferred_element_type=jnp.float32)
    tok_dev = tok_seq // lax.axis_size("exp")
    own_start = lax.axis_index("exp") * tok_dev
    n_exp = lax.axis_size("exp")
    exp_index = lax.axis_index("exp")
    section_sum = partial_value + lax.ppermute(
        partial_value.astype(jnp.bfloat16), "section", swap
    ).astype(jnp.float32)
    summed = jnp.where(
        section_index == 0,
        lax.dynamic_slice_in_dim(section_sum, own_start, tok_dev, 0),
        jnp.zeros((tok_dev, width), jnp.float32),
    )
    for step in range(n_exp // 2):
        pairs = []
        for core in range(2):
            shift = 2 * step + 1 + core
            if shift < n_exp:
                pairs += [(core * n_exp + j, core * n_exp + (j + shift) % n_exp) for j in range(n_exp)]
        target = (exp_index + 2 * step + 1 + section_index) % n_exp
        chunk = lax.dynamic_slice_in_dim(section_sum, target * tok_dev, tok_dev, 0)
        summed = summed + lax.ppermute(
            chunk.astype(jnp.bfloat16), ("section", "exp"), pairs
        ).astype(jnp.float32)
    summed = summed + lax.ppermute(summed, "section", swap)
    own_rows = lax.dynamic_slice_in_dim(hidden_in, own_start, tok_dev, 0)
    residual = (own_rows.astype(jnp.float32) + summed).astype(jnp.bfloat16)
    moe_in = rms_scale(residual, moe_gain)
    experts = lax.axis_size("seq") * lax.axis_size("exp") // 2
    top_count = expert_ids.shape[1]
    capacity = min(tok_dev, max(2, 2 * tok_dev * top_count // experts))
    row_count = tok_dev * top_count
    flat_ids = expert_ids.reshape(row_count)
    one_hot = (flat_ids[:, None] == jnp.arange(experts, dtype=jnp.int32)[None, :]).astype(jnp.int32)
    slot_rank = jnp.sum((jnp.cumsum(one_hot, axis=0) - one_hot) * one_hot, axis=1)
    slot_index = flat_ids * capacity + slot_rank
    placed = slot_index[:, None] == jnp.arange(experts * capacity, dtype=jnp.int32)[None, :]
    repeated = jnp.repeat(moe_in, top_count, axis=0)
    outgoing = lax.dot_general(
        placed.astype(jnp.bfloat16),
        repeated,
        (((0,), (0,)), ((), ())),
        preferred_element_type=jnp.float32,
    ).astype(jnp.bfloat16)
    row_token = jnp.arange(row_count, dtype=jnp.int32) // top_count
    token_hot = (row_token[None, :] == jnp.arange(tok_dev, dtype=jnp.int32)[:, None]).astype(
        jnp.float32
    )
    weighted = token_hot * route_weights.reshape(row_count)[None, :]
    combine = jnp.dot(weighted, placed.astype(jnp.float32), precision=lax.Precision.HIGHEST)
    half_cap = capacity // 2
    own_half = lax.dynamic_slice_in_dim(
        outgoing.reshape(experts, capacity, width), section_index * half_cap, half_cap, 1
    )
    doubled = jnp.broadcast_to(
        own_half.reshape(experts, 1, half_cap, width), (experts, 2, half_cap, width)
    ).reshape(2 * experts, half_cap, width)
    arrived = lax.all_to_all(doubled, ("seq", "exp"), split_axis=0, concat_axis=0, tiled=True)
    partner = lax.ppermute(arrived, "section", [(0, 1), (1, 0)])

    def quarter_ffn(rows):
        gate_proj = jnp.dot(rows, gate_halves[0], preferred_element_type=jnp.float32)
        up_proj = jnp.dot(rows, up_halves[0], preferred_element_type=jnp.float32)
        activated = (jax.nn.silu(gate_proj) * up_proj).astype(jnp.bfloat16)
        return jnp.dot(activated, down_halves[0], preferred_element_type=jnp.float32).astype(
            jnp.bfloat16
        )

    own_rows_out = quarter_ffn(arrived.reshape(-1, width))
    own_rows_out, partner = lax.optimization_barrier((own_rows_out, partner))
    partner_rows_out = quarter_ffn(partner.reshape(-1, width))
    pair_sum = own_rows_out.astype(jnp.float32) + lax.ppermute(
        partner_rows_out, "section", [(0, 1), (1, 0)]
    ).astype(jnp.float32)
    returned = lax.all_to_all(
        pair_sum.astype(jnp.bfloat16).reshape(arrived.shape),
        ("seq", "exp"),
        split_axis=0,
        concat_axis=0,
        tiled=True,
    )
    halves_sum = jnp.sum(
        returned.reshape(experts, 2, half_cap, width).astype(jnp.float32), axis=1
    ).reshape(experts * half_cap, width)
    own_combine = lax.dynamic_slice_in_dim(
        combine.reshape(tok_dev, experts, capacity), section_index * half_cap, half_cap, 2
    ).reshape(tok_dev, experts * half_cap)
    moe_part = jnp.dot(own_combine, halves_sum, precision=lax.Precision.HIGHEST)
    moe_total = moe_part + lax.ppermute(moe_part, "section", [(0, 1), (1, 0)])
    return (residual.astype(jnp.float32) + moe_total).astype(jnp.bfloat16)


def solution(mesh):
    in_specs = (
        P("seq", None),
        P("seq"),
        P(),
        P(None, ("section", "exp")),
        P(None, ("section", "exp")),
        P(None, ("section", "exp")),
        P(("section", "exp"), None),
        P(),
        P(("seq", "exp"), None),
        P(("seq", "exp"), None),
        P(("seq", "exp"), None, "section"),
        P(("seq", "exp"), None, "section"),
        P(("seq", "exp"), "section", None),
    )
    out_specs = P(("seq", "exp"), None)
    return jax.shard_map(
        per_device, mesh=mesh, in_specs=in_specs, out_specs=out_specs, check_vma=False
    )
```
